32 devices in a mesh: bucket: 4 (over y, x), group: 8 (over z, core).
Axes of the slice: x: 2, y: 2, z: 4, core: 2. Of those that a mesh axis runs over, the one named last changes fastest.
Arguments:
- embeddings: bfloat16 [4, 8, 4, 128, 768], P('bucket', 'group'), may hold values from -6 to 6
- counts: int32 [4, 8, 4, 1], P('bucket', 'group'), may hold values from 42 to 128, as said below
Outputs:
- neighbour_sums: bfloat16 [4, 8, 512, 768], P('bucket', 'group')
The draws below stay inside these ranges and needn't reach their ends.
Inputs may be any that keep to these rules, and one draw needn't show every extreme that they name: `counts`: each count is a live prefix of its 128 slots; in every draw some slot range is full.
All inputs are finite; a program needn't handle non-finite values.
Results may differ from the reference program's by a relative error of at most 0.0052.
Values may be sent and summed in bfloat16 or wider, within the bound.
No kernel may reach another device: no remote copies, remote signals or barrier semaphores. Data moves between devices by JAX's collectives and lax.ppermute only.
A program may use at most 128 MiB of HBM per device.

```python
import jax
import jax.numpy as jnp
from jax import lax

D = 768
SLOT = 128
ROUNDS = 4
BUCKETS = 4
BLOCKS = 8
ROWS = 512


def draw_counts(key, part):
    first, second = jax.random.split(key)
    base = jax.random.randint(first, (BUCKETS, BLOCKS, BUCKETS, 1), SLOT // 3, SLOT + 1)
    spot = jax.random.randint(second, (), 0, BUCKETS * BLOCKS * BUCKETS)
    flat = base.reshape(-1)
    flat = jnp.where(jnp.arange(flat.shape[0]) == spot, SLOT, flat)
    return flat.reshape(base.shape).astype(jnp.int32)


def block_levels(own_key, extent, cuts, least, largest):
    factor_of, own = 1.0, jax.random.fold_in(own_key, 6)
    for position, shards_of in cuts:
        steps = jnp.exp(jax.random.uniform(jax.random.fold_in(own, position), (shards_of,), jnp.float32, least / len(cuts), largest / len(cuts)))
        factor_of = factor_of * jnp.repeat(steps, extent[position] // shards_of).reshape([-1 if axis == position else 1 for axis in range(len(extent))])
    return factor_of


def normal_values(own_key, shape, scale, limit, pieces=(), held_as=jnp.bfloat16):
    factor_of = block_levels(own_key, shape, pieces, -0.22, 0.18) if pieces else 1.0
    entries = jax.random.normal(own_key, shape, jnp.float32) * scale * factor_of
    return jnp.minimum(jnp.maximum(entries, -limit), limit).astype(held_as)


def setup_inputs(seed: int = 0) -> dict:
    streams_of = jax.random.split(jax.random.key(seed), 3)
    embeddings = normal_values(streams_of[0], (BUCKETS, BLOCKS, BUCKETS, SLOT, D), 1.0, 6.0, ((0, 4), (1, 8)))
    counts = draw_counts(jax.random.fold_in(streams_of[2], 71), 0)
    return dict(embeddings=embeddings, counts=counts)


EPS = 1e-06
TEMP = 12.0

def normalize(block):
    values = block.astype(jnp.float32)
    return (values * lax.rsqrt(lax.optimization_barrier(jnp.sum(values * values, axis=-1, keepdims=True)) + EPS)).astype(jnp.bfloat16)

def pair_terms(unit_a, unit_b, data_b, live_b, extra):
    scores = jnp.dot(unit_a, unit_b.T, preferred_element_type=jnp.float32)
    weights = jnp.exp(TEMP * scores) * live_b[None, :] * extra
    summed = jnp.dot(weights.astype(jnp.bfloat16), data_b, preferred_element_type=jnp.float32)
    return (summed, lax.optimization_barrier(jnp.sum(weights * weights, axis=1)))

def reference(embeddings, counts):
    x_all = jnp.transpose(embeddings, (2, 1, 0, 3, 4)).reshape(BUCKETS, BLOCKS, ROWS, D)
    slots = jnp.arange(SLOT, dtype=jnp.int32)[None, None, None, :]
    live_all = (slots < counts).astype(jnp.float32)
    live_all = jnp.transpose(live_all, (2, 1, 0, 3)).reshape(BUCKETS, BLOCKS, ROWS)
    u_all = normalize(x_all)
    not_self = 1.0 - jnp.eye(ROWS, dtype=jnp.float32)
    ones = jnp.ones((ROWS, ROWS), jnp.float32)

    def one(index):
        bucket = index // BLOCKS
        block = index % BLOCKS
        unit_a = u_all[bucket, block]
        summed, squares = pair_terms(unit_a, unit_a, x_all[bucket, block], live_all[bucket, block], not_self)
        for dist in range(1, ROUNDS + 1):
            for sign in (1, -1):
                other = ((block + sign * dist) % BLOCKS).astype(jnp.int32)
                part_sum, part_sq = pair_terms(unit_a, u_all[bucket, other], x_all[bucket, other], live_all[bucket, other], ones)
                summed = summed + part_sum
                squares = squares + part_sq
        result = summed * lax.rsqrt(squares)[:, None] * live_all[bucket, block][:, None]
        return result.astype(jnp.bfloat16)
    outputs = lax.map(one, jnp.arange(BUCKETS * BLOCKS, dtype=jnp.int32))
    return outputs.reshape(BUCKETS, BLOCKS, ROWS, D)
```

```python
import jax
import jax.numpy as jnp
from jax import lax
from jax.sharding import Mesh, PartitionSpec as P

ROUNDS = 4


EPS = 1e-06
TEMP = 12.0
CORES = 2


def normalize(block):
    values = block.astype(jnp.float32)
    return (values * lax.rsqrt(jnp.sum(values * values, axis=-1, keepdims=True) + EPS)).astype(
        jnp.bfloat16
    )


def weigh(unit_a, unit_b, live_b, extra):
    scores = jnp.dot(unit_a, unit_b.T, preferred_element_type=jnp.float32)
    return jnp.exp(TEMP * scores) * live_b[None, :] * extra


def per_device(embeddings, counts):
    all_counts = lax.all_gather(counts, ("bucket", "chip", "core"), axis=0, tiled=True)
    slabs = lax.all_to_all(embeddings, "bucket", split_axis=2, concat_axis=0, tiled=True)
    sources = slabs.shape[0]
    slot_rows = slabs.shape[3]
    width = slabs.shape[4]
    rows = sources * slot_rows
    data = slabs.reshape(rows, width)
    bucket = lax.axis_index("bucket")
    chips = lax.axis_size("chip")
    cores = lax.axis_size("core")
    blocks = chips * cores
    position = lax.axis_index("chip") * cores + lax.axis_index("core")
    all_counts = all_counts.reshape(sources, blocks, counts.shape[2])
    mine = lax.dynamic_index_in_dim(all_counts, bucket, axis=2, keepdims=False)
    block_counts = mine.T
    slot_index = lax.broadcasted_iota(jnp.int32, (blocks, sources, slot_rows), 2)
    all_live = (slot_index < block_counts[:, :, None]).astype(jnp.float32).reshape(blocks, rows)
    live = lax.dynamic_index_in_dim(all_live, position, axis=0, keepdims=False)
    unit = normalize(data)
    not_self = 1.0 - jnp.eye(rows, dtype=jnp.float32)
    own = weigh(unit, unit, live, not_self)
    summed = jnp.dot(own.astype(jnp.bfloat16), data, preferred_element_type=jnp.float32)
    squares = jnp.sum(own * own, axis=1)
    along = lax.all_gather(data, "chip", axis=0, tiled=False)
    both = lax.all_gather(along, "core", axis=1, tiled=False)
    all_data = both.reshape(blocks * rows, width)
    for dist in range(1, ROUNDS + 1):
        for sign in (1, -1):
            other = (position + sign * dist) % blocks
            start = other * rows
            got_data = lax.dynamic_slice_in_dim(all_data, start, rows, 0)
            got_live = lax.dynamic_index_in_dim(all_live, other, axis=0, keepdims=False)
            weights = weigh(unit, normalize(got_data), got_live, 1.0)
            summed = summed + jnp.dot(
                weights.astype(jnp.bfloat16), got_data, preferred_element_type=jnp.float32
            )
            squares = squares + jnp.sum(weights * weights, axis=1)
    result = summed * lax.rsqrt(squares)[:, None] * live[:, None]
    return result.astype(jnp.bfloat16).reshape(1, 1, rows, width)


def solution(mesh):
    devices = mesh.devices
    split = Mesh(
        devices.reshape(devices.shape[0], devices.shape[1] // CORES, CORES),
        ("bucket", "chip", "core"),
    )
    group = ("chip", "core")
    in_specs = (P("bucket", group, None, None, None), P("bucket", group, None, None))
    out_specs = P("bucket", group, None, None)
    return jax.shard_map(
        per_device, mesh=split, in_specs=in_specs, out_specs=out_specs, check_vma=False
    )
```

```python
import jax
import jax.numpy as jnp
from jax import lax
from jax.sharding import Mesh, PartitionSpec as P

ROUNDS = 4


EPS = 1e-06
TEMP = 12.0
CORES = 2


def normalize(block):
    values = block.astype(jnp.float32)
    return (values * lax.rsqrt(jnp.sum(values * values, axis=-1, keepdims=True) + EPS)).astype(
        jnp.bfloat16
    )


def weigh(unit_a, unit_b, live_b, extra):
    scores = jnp.dot(unit_a, unit_b.T, preferred_element_type=jnp.float32)
    return jnp.exp(TEMP * scores) * live_b[None, :] * extra


def live_of(block_counts, slot_rows):
    sources = block_counts.shape[0]
    slot_index = lax.broadcasted_iota(jnp.int32, (sources, slot_rows), 1)
    return (slot_index < block_counts.reshape(sources, 1)).astype(jnp.float32).reshape(-1)


def per_device(embeddings, counts):
    slabs, slab_counts = (
        lax.all_to_all(embeddings, "bucket", split_axis=2, concat_axis=0, tiled=True),
        lax.all_to_all(counts, "bucket", split_axis=2, concat_axis=0, tiled=True),
    )
    sources = slabs.shape[0]
    slot_rows = slabs.shape[3]
    width = slabs.shape[4]
    rows = sources * slot_rows
    data = slabs.reshape(rows, width)
    own_counts = slab_counts.reshape(sources)
    live = live_of(own_counts, slot_rows)
    chips = lax.axis_size("chip")
    cores = lax.axis_size("core")
    blocks = chips * cores
    chip = lax.axis_index("chip")
    core = lax.axis_index("core")
    position = chip * cores + core

    unit = normalize(data)
    not_self = 1.0 - jnp.eye(rows, dtype=jnp.float32)
    own = weigh(unit, unit, live, not_self)
    summed = jnp.dot(own.astype(jnp.bfloat16), data, preferred_element_type=jnp.float32)
    squares = jnp.sum(own * own, axis=1)

    def times_listed(other_chip, other_core):
        block = other_chip * cores + other_core
        listed = jnp.int32(0)
        for dist in range(1, ROUNDS + 1):
            for sign in (1, -1):
                listed = listed + (((position + sign * dist) % blocks) == block).astype(jnp.int32)
        exists = (other_chip >= 0) & (other_chip < chips)
        return jnp.where(exists, listed, 0).astype(jnp.float32)

    def add_pair(acc, got, weight):
        summed, squares = acc
        got_data = got[:rows]
        got_counts = got[rows, :sources].astype(jnp.int32)
        weights = weigh(unit, normalize(got_data), live_of(got_counts, slot_rows), 1.0)
        part = jnp.dot(weights.astype(jnp.bfloat16), got_data, preferred_element_type=jnp.float32)
        return (summed + weight * part, squares + weight * jnp.sum(weights * weights, axis=1))

    swap = [(c, (c + 1) % cores) for c in range(cores)]
    up = [(c, c + 1) for c in range(chips - 1)]
    down = [(c + 1, c) for c in range(chips - 1)]
    acc = (summed, squares)
    tail = jnp.zeros((16, width), jnp.bfloat16).at[0, :sources].set(own_counts.astype(jnp.bfloat16))
    mine = jnp.concatenate([data, tail], axis=0)
    other_core = (core + 1) % cores
    swapped = lax.ppermute(mine, "core", swap)
    acc = add_pair(acc, swapped, times_listed(chip, other_core))
    from_below, from_above = mine, mine
    for step in range(1, chips):
        from_below = lax.ppermute(from_below, "chip", up)
        from_above = lax.ppermute(from_above, "chip", down)
        below_swapped = lax.ppermute(from_below, "core", swap)
        above_swapped = lax.ppermute(from_above, "core", swap)
        acc = add_pair(acc, from_below, times_listed(chip - step, core))
        acc = add_pair(acc, from_above, times_listed(chip + step, core))
        acc = add_pair(acc, below_swapped, times_listed(chip - step, other_core))
        acc = add_pair(acc, above_swapped, times_listed(chip + step, other_core))
    summed, squares = acc
    result = summed * lax.rsqrt(squares)[:, None] * live[:, None]
    return result.astype(jnp.bfloat16).reshape(1, 1, rows, width)


def solution(mesh):
    devices = mesh.devices
    split = Mesh(
        devices.reshape(devices.shape[0], devices.shape[1] // CORES, CORES),
        ("bucket", "chip", "core"),
    )
    group = ("chip", "core")
    in_specs = (P("bucket", group, None, None, None), P("bucket", group, None, None))
    out_specs = P("bucket", group, None, None)
    return jax.shard_map(
        per_device, mesh=split, in_specs=in_specs, out_specs=out_specs, check_vma=False
    )
```

```python
import jax
import jax.numpy as jnp
from jax import lax
from jax.sharding import Mesh, PartitionSpec as P

ROUNDS = 4


EPS = 1e-06
TEMP = 12.0
CORES = 2


def normalize(block):
    values = block.astype(jnp.float32)
    return (values * lax.rsqrt(jnp.sum(values * values, axis=-1, keepdims=True) + EPS)).astype(
        jnp.bfloat16
    )


def weigh(unit_a, unit_b, live_b, extra):
    scores = jnp.dot(unit_a, unit_b.T, preferred_element_type=jnp.float32)
    return jnp.exp(TEMP * scores) * live_b[None, :] * extra


def live_of(block_counts, slot_rows):
    sources = block_counts.shape[0]
    slot_index = lax.broadcasted_iota(jnp.int32, (sources, slot_rows), 1)
    return (slot_index < block_counts.reshape(sources, 1)).astype(jnp.float32).reshape(-1)


def per_device(embeddings, counts):
    slot_rows = embeddings.shape[3]
    width = embeddings.shape[4]
    count_rows = jnp.zeros(embeddings.shape[:3] + (16, width), jnp.bfloat16)
    count_rows = count_rows.at[:, :, :, 0, 0].set(counts[..., 0].astype(jnp.bfloat16))
    packed = jnp.concatenate([embeddings, count_rows], axis=3)
    slabs = lax.all_to_all(packed, "bucket", split_axis=2, concat_axis=0, tiled=True)
    sources = slabs.shape[0]
    rows = sources * slot_rows
    data = slabs[:, :, :, :slot_rows].reshape(rows, width)
    own_counts = slabs[:, 0, 0, slot_rows, 0].astype(jnp.int32)
    live = live_of(own_counts, slot_rows)
    chips = lax.axis_size("chip")
    cores = lax.axis_size("core")
    blocks = chips * cores
    chip = lax.axis_index("chip")
    core = lax.axis_index("core")
    position = chip * cores + core

    unit = normalize(data)
    not_self = 1.0 - jnp.eye(rows, dtype=jnp.float32)
    own = weigh(unit, unit, live, not_self)
    summed = jnp.dot(own.astype(jnp.bfloat16), data, preferred_element_type=jnp.float32)
    squares = jnp.sum(own * own, axis=1)

    def times_listed(other_chip, other_core):
        block = other_chip * cores + other_core
        listed = jnp.int32(0)
        for dist in range(1, ROUNDS + 1):
            for sign in (1, -1):
                listed = listed + (((position + sign * dist) % blocks) == block).astype(jnp.int32)
        exists = (other_chip >= 0) & (other_chip < chips)
        return jnp.where(exists, listed, 0).astype(jnp.float32)

    def add_pair(acc, got, weight):
        summed, squares = acc
        got_data = got[:rows]
        got_counts = got[rows, :sources].astype(jnp.int32)
        weights = weigh(unit, normalize(got_data), live_of(got_counts, slot_rows), 1.0)
        part = jnp.dot(weights.astype(jnp.bfloat16), got_data, preferred_element_type=jnp.float32)
        return (summed + weight * part, squares + weight * jnp.sum(weights * weights, axis=1))

    swap = [(c, (c + 1) % cores) for c in range(cores)]
    up = [(c, c + 1) for c in range(chips - 1)]
    down = [(c + 1, c) for c in range(chips - 1)]
    acc = (summed, squares)
    tail = jnp.zeros((16, width), jnp.bfloat16).at[0, :sources].set(own_counts.astype(jnp.bfloat16))
    mine = jnp.concatenate([data, tail], axis=0)
    other_core = (core + 1) % cores
    swapped = lax.ppermute(mine, "core", swap)
    acc = add_pair(acc, swapped, times_listed(chip, other_core))
    from_below, from_above = mine, mine
    for step in range(1, chips):
        from_below = lax.ppermute(from_below, "chip", up)
        from_above = lax.ppermute(from_above, "chip", down)
        below_swapped = lax.ppermute(from_below, "core", swap)
        above_swapped = lax.ppermute(from_above, "core", swap)
        acc = add_pair(acc, from_below, times_listed(chip - step, core))
        acc = add_pair(acc, from_above, times_listed(chip + step, core))
        acc = add_pair(acc, below_swapped, times_listed(chip - step, other_core))
        acc = add_pair(acc, above_swapped, times_listed(chip + step, other_core))
    summed, squares = acc
    result = summed * lax.rsqrt(squares)[:, None] * live[:, None]
    return result.astype(jnp.bfloat16).reshape(1, 1, rows, width)


def solution(mesh):
    devices = mesh.devices
    split = Mesh(
        devices.reshape(devices.shape[0], devices.shape[1] // CORES, CORES),
        ("bucket", "chip", "core"),
    )
    group = ("chip", "core")
    in_specs = (P("bucket", group, None, None, None), P("bucket", group, None, None))
    out_specs = P("bucket", group, None, None)
    return jax.shard_map(
        per_device, mesh=split, in_specs=in_specs, out_specs=out_specs, check_vma=False
    )
```

```python
import jax
import jax.numpy as jnp
from jax import lax
from jax.sharding import Mesh, PartitionSpec as P

ROUNDS = 4


EPS = 1e-06
TEMP = 12.0
CORES = 2


def normalize(block):
    values = block.astype(jnp.float32)
    return (values * lax.rsqrt(jnp.sum(values * values, axis=-1, keepdims=True) + EPS)).astype(
        jnp.bfloat16
    )


def weigh(unit_a, unit_b, live_b, extra):
    scores = jnp.dot(unit_a, unit_b.T, preferred_element_type=jnp.float32)
    return jnp.exp(TEMP * scores) * live_b[None, :] * extra


def live_of(block_counts, slot_rows):
    sources = block_counts.shape[0]
    slot_index = lax.broadcasted_iota(jnp.int32, (sources, slot_rows), 1)
    return (slot_index < block_counts.reshape(sources, 1)).astype(jnp.float32).reshape(-1)


def per_device(embeddings, counts):
    slot_rows = embeddings.shape[3]
    width = embeddings.shape[4]
    count_rows = jnp.zeros(embeddings.shape[:3] + (16, width), jnp.bfloat16)
    count_rows = count_rows.at[:, :, :, 0, 0].set(counts[..., 0].astype(jnp.bfloat16))
    packed = jnp.concatenate([embeddings, count_rows], axis=3)
    slabs = lax.all_to_all(packed, "bucket", split_axis=2, concat_axis=0, tiled=True)
    sources = slabs.shape[0]
    rows = sources * slot_rows
    data = slabs[:, :, :, :slot_rows].reshape(rows, width)
    own_counts = slabs[:, 0, 0, slot_rows, 0].astype(jnp.int32)
    live = live_of(own_counts, slot_rows)
    chips = lax.axis_size("chip")
    cores = lax.axis_size("core")
    blocks = chips * cores
    chip = lax.axis_index("chip")
    core = lax.axis_index("core")
    position = chip * cores + core

    unit = normalize(data)
    not_self = 1.0 - jnp.eye(rows, dtype=jnp.float32)
    own = weigh(unit, unit, live, not_self)
    summed = jnp.dot(own.astype(jnp.bfloat16), data, preferred_element_type=jnp.float32)
    squares = jnp.sum(own * own, axis=1)

    def times_listed(other_chip, other_core):
        block = other_chip * cores + other_core
        listed = jnp.int32(0)
        for dist in range(1, ROUNDS + 1):
            for sign in (1, -1):
                listed = listed + (((position + sign * dist) % blocks) == block).astype(jnp.int32)
        exists = (other_chip >= 0) & (other_chip < chips)
        return jnp.where(exists, listed, 0).astype(jnp.float32)

    def pair_terms(acc, got, weight):
        summed, squares = acc
        got_data = got[:rows]
        got_counts = got[rows, :sources].astype(jnp.int32)
        weights = weigh(unit, normalize(got_data), live_of(got_counts, slot_rows), 1.0)
        part = jnp.dot(weights.astype(jnp.bfloat16), got_data, preferred_element_type=jnp.float32)
        return (summed + weight * part, squares + weight * jnp.sum(weights * weights, axis=1))

    def add_pair(acc, got, weight):
        return lax.cond(weight > 0, pair_terms, lambda acc, got, weight: acc, acc, got, weight)

    swap = [(c, (c + 1) % cores) for c in range(cores)]
    up = [(c, c + 1) for c in range(chips - 1)]
    down = [(c + 1, c) for c in range(chips - 1)]
    acc = (summed, squares)
    tail = jnp.zeros((16, width), jnp.bfloat16).at[0, :sources].set(own_counts.astype(jnp.bfloat16))
    mine = jnp.concatenate([data, tail], axis=0)
    other_core = (core + 1) % cores
    received = (lax.ppermute(mine, "chip", up), lax.ppermute(mine, "chip", down))
    swapped = lax.ppermute(mine, "core", swap)
    acc = add_pair(acc, swapped, times_listed(chip, other_core))
    for step in range(1, chips):
        acc, received = lax.optimization_barrier((acc, received))
        from_below, from_above = received
        if step + 1 < chips:
            received = (lax.ppermute(from_below, "chip", up), lax.ppermute(from_above, "chip", down))
        below_swapped = lax.ppermute(from_below, "core", swap)
        above_swapped = lax.ppermute(from_above, "core", swap)
        acc = add_pair(acc, from_below, times_listed(chip - step, core))
        acc = add_pair(acc, from_above, times_listed(chip + step, core))
        acc = add_pair(acc, below_swapped, times_listed(chip - step, other_core))
        acc = add_pair(acc, above_swapped, times_listed(chip + step, other_core))
    summed, squares = acc
    result = summed * lax.rsqrt(squares)[:, None] * live[:, None]
    return result.astype(jnp.bfloat16).reshape(1, 1, rows, width)


def solution(mesh):
    devices = mesh.devices
    split = Mesh(
        devices.reshape(devices.shape[0], devices.shape[1] // CORES, CORES),
        ("bucket", "chip", "core"),
    )
    group = ("chip", "core")
    in_specs = (P("bucket", group, None, None, None), P("bucket", group, None, None))
    out_specs = P("bucket", group, None, None)
    return jax.shard_map(
        per_device, mesh=split, in_specs=in_specs, out_specs=out_specs, check_vma=False
    )
```

```python
import jax
import jax.numpy as jnp
from jax import lax
from jax.sharding import Mesh, PartitionSpec as P

ROUNDS = 4


EPS = 1e-06
TEMP = 12.0
CORES = 2


def normalize(block):
    values = block.astype(jnp.float32)
    return (values * lax.rsqrt(jnp.sum(values * values, axis=-1, keepdims=True) + EPS)).astype(
        jnp.bfloat16
    )


def weigh(unit_a, unit_b, live_b, extra):
    scores = jnp.dot(unit_a, unit_b.T, preferred_element_type=jnp.float32)
    return jnp.exp(TEMP * scores) * live_b[None, :] * extra


def live_of(block_counts, slot_rows):
    sources = block_counts.shape[0]
    slot_index = lax.broadcasted_iota(jnp.int32, (sources, slot_rows), 1)
    return (slot_index < block_counts.reshape(sources, 1)).astype(jnp.float32).reshape(-1)


def per_device(embeddings, counts):
    slot_rows = embeddings.shape[3]
    width = embeddings.shape[4]
    count_rows = jnp.zeros(embeddings.shape[:3] + (16, width), jnp.bfloat16)
    count_rows = count_rows.at[:, :, :, 0, 0].set(counts[..., 0].astype(jnp.bfloat16))
    packed = jnp.concatenate([embeddings, count_rows], axis=3)
    slabs = lax.all_to_all(packed, "bucket", split_axis=2, concat_axis=0, tiled=True)
    sources = slabs.shape[0]
    rows = sources * slot_rows
    data = slabs[:, :, :, :slot_rows].reshape(rows, width)
    own_counts = slabs[:, 0, 0, slot_rows, 0].astype(jnp.int32)
    live = live_of(own_counts, slot_rows)
    chips = lax.axis_size("chip")
    cores = lax.axis_size("core")
    blocks = chips * cores
    chip = lax.axis_index("chip")
    core = lax.axis_index("core")
    position = chip * cores + core

    unit = normalize(data)
    not_self = 1.0 - jnp.eye(rows, dtype=jnp.float32)
    own = weigh(unit, unit, live, not_self)
    summed = jnp.dot(own.astype(jnp.bfloat16), data, preferred_element_type=jnp.float32)
    squares = jnp.sum(own * own, axis=1)

    def times_listed(other_chip, other_core):
        block = other_chip * cores + other_core
        listed = jnp.int32(0)
        for dist in range(1, ROUNDS + 1):
            for sign in (1, -1):
                listed = listed + (((position + sign * dist) % blocks) == block).astype(jnp.int32)
        exists = (other_chip >= 0) & (other_chip < chips)
        return jnp.where(exists, listed, 0).astype(jnp.float32)

    def pair_terms(acc, got, weight):
        summed, squares = acc
        got_data = got[:rows]
        got_counts = got[rows, :sources].astype(jnp.int32)
        weights = weigh(unit, normalize(got_data), live_of(got_counts, slot_rows), 1.0)
        part = jnp.dot(weights.astype(jnp.bfloat16), got_data, preferred_element_type=jnp.float32)
        return (summed + weight * part, squares + weight * jnp.sum(weights * weights, axis=1))

    def add_pair(acc, got, weight):
        return pair_terms(acc, got, weight)

    swap = [(c, (c + 1) % cores) for c in range(cores)]
    up = [(c, c + 1) for c in range(chips - 1)]
    down = [(c + 1, c) for c in range(chips - 1)]
    acc = (summed, squares)
    tail = jnp.zeros((16, width), jnp.bfloat16).at[0, :sources].set(own_counts.astype(jnp.bfloat16))
    mine = jnp.concatenate([data, tail], axis=0)
    other_core = (core + 1) % cores
    received = (lax.ppermute(mine, "chip", up), lax.ppermute(mine, "chip", down))
    swapped = lax.ppermute(mine, "core", swap)
    acc = add_pair(acc, swapped, times_listed(chip, other_core))
    for step in range(1, chips):
        acc, received = lax.optimization_barrier((acc, received))
        from_below, from_above = received
        if step + 2 < chips:
            received = (lax.ppermute(from_below, "chip", up), lax.ppermute(from_above, "chip", down))
        elif step + 2 == chips and chips >= 4:
            ends = [(chips - 2, chips - 1), (1, 0)]
            outgoing = jnp.where(chip == chips - 2, from_below, from_above)
            last = lax.ppermute(outgoing, "chip", ends)
            received = (last, last)
        elif step + 2 == chips:
            received = (lax.ppermute(from_below, "chip", up), lax.ppermute(from_above, "chip", down))
        if step + 1 == chips and chips >= 4:
            far_chip = jnp.where(chip == 0, chips - 1, jnp.where(chip == chips - 1, 0, -1))
            far_swapped = lax.ppermute(from_below, "core", swap)
            acc = add_pair(acc, from_below, times_listed(far_chip, core))
            acc = add_pair(acc, far_swapped, times_listed(far_chip, other_core))
            continue
        below_swapped = lax.ppermute(from_below, "core", swap)
        above_swapped = lax.ppermute(from_above, "core", swap)
        acc = add_pair(acc, from_below, times_listed(chip - step, core))
        acc = add_pair(acc, from_above, times_listed(chip + step, core))
        acc = add_pair(acc, below_swapped, times_listed(chip - step, other_core))
        acc = add_pair(acc, above_swapped, times_listed(chip + step, other_core))
    summed, squares = acc
    result = summed * lax.rsqrt(squares)[:, None] * live[:, None]
    return result.astype(jnp.bfloat16).reshape(1, 1, rows, width)


def solution(mesh):
    devices = mesh.devices
    split = Mesh(
        devices.reshape(devices.shape[0], devices.shape[1] // CORES, CORES),
        ("bucket", "chip", "core"),
    )
    group = ("chip", "core")
    in_specs = (P("bucket", group, None, None, None), P("bucket", group, None, None))
    out_specs = P("bucket", group, None, None)
    return jax.shard_map(
        per_device, mesh=split, in_specs=in_specs, out_specs=out_specs, check_vma=False
    )
```

```python
import jax
import jax.numpy as jnp
from jax import lax
from jax.sharding import Mesh, PartitionSpec as P

ROUNDS = 4


EPS = 1e-06
TEMP = 12.0
CORES = 2
COUNT_ROWS = 16


def normalize(block):
    values = block.astype(jnp.float32)
    return (values * lax.rsqrt(jnp.sum(values * values, axis=-1, keepdims=True) + EPS)).astype(
        jnp.bfloat16
    )


def weigh(unit_a, unit_b, live_b, extra):
    scores = jnp.dot(unit_a, unit_b.T, preferred_element_type=jnp.float32)
    return jnp.exp(TEMP * scores) * live_b[None, :] * extra


def split_pieces(pieces, slot_rows):
    n, _, width = pieces.shape
    data = pieces[:, :slot_rows].reshape(n * slot_rows, width)
    piece_counts = pieces[:, slot_rows, 0].astype(jnp.int32)
    slot_index = lax.broadcasted_iota(jnp.int32, (n, slot_rows), 1)
    live = (slot_index < piece_counts[:, None]).astype(jnp.float32).reshape(-1)
    return data, live


def per_device(embeddings, counts):
    buckets = lax.axis_size("bucket")
    bucket = lax.axis_index("bucket")
    slot_rows = embeddings.shape[3]
    width = embeddings.shape[4]
    count_rows = jnp.zeros(embeddings.shape[2:3] + (COUNT_ROWS, width), jnp.bfloat16)
    count_rows = count_rows.at[:, 0, 0].set(counts[0, 0, :, 0].astype(jnp.bfloat16))
    packed = jnp.concatenate([embeddings[0, 0], count_rows], axis=1)

    arrived = [lax.dynamic_index_in_dim(packed, bucket, axis=0, keepdims=False)]
    for m in range(1, buckets):
        outgoing = lax.dynamic_index_in_dim(packed, bucket ^ m, axis=0, keepdims=False)
        arrived.append(lax.ppermute(outgoing, "bucket", [(i, i ^ m) for i in range(buckets)]))
    half = buckets // 2
    halves = [jnp.stack(arrived[:half]), jnp.stack(arrived[half:])]

    own_data, live = split_pieces(jnp.stack(arrived), slot_rows)
    rows = own_data.shape[0]
    chips = lax.axis_size("chip")
    cores = lax.axis_size("core")
    blocks = chips * cores
    chip = lax.axis_index("chip")
    core = lax.axis_index("core")
    position = chip * cores + core
    other_core = (core + 1) % cores

    unit = normalize(own_data)
    not_self = 1.0 - jnp.eye(rows, dtype=jnp.float32)
    own = weigh(unit, unit, live, not_self)
    summed = jnp.dot(own.astype(jnp.bfloat16), own_data, preferred_element_type=jnp.float32)
    squares = jnp.sum(own * own, axis=1)
    acc = (summed, squares)

    def times_listed(other_chip, other_core):
        block = other_chip * cores + other_core
        listed = jnp.int32(0)
        for dist in range(1, ROUNDS + 1):
            for sign in (1, -1):
                listed = listed + (((position + sign * dist) % blocks) == block).astype(jnp.int32)
        exists = (other_chip >= 0) & (other_chip < chips)
        return jnp.where(exists, listed, 0).astype(jnp.float32)

    def add_pair(acc, got, weight):
        summed, squares = acc
        got_data, got_live = split_pieces(got, slot_rows)
        weights = weigh(unit, normalize(got_data), got_live, 1.0)
        part = jnp.dot(weights.astype(jnp.bfloat16), got_data, preferred_element_type=jnp.float32)
        return (summed + weight * part, squares + weight * jnp.sum(weights * weights, axis=1))

    swap = [(c, (c + 1) % cores) for c in range(cores)]
    up = [(c, c + 1) for c in range(chips - 1)]
    down = [(c + 1, c) for c in range(chips - 1)]
    ends = chips >= 4

    def relay(piece):
        yield lax.ppermute(piece, "core", swap), times_listed(chip, other_core)
        from_below, from_above = piece, piece
        for step in range(1, chips):
            if ends and step + 1 == chips:
                outgoing = jnp.where(chip == chips - 2, from_below, from_above)
                far = lax.ppermute(outgoing, "chip", [(chips - 2, chips - 1), (1, 0)])
                far_chip = jnp.where(chip == 0, chips - 1, jnp.where(chip == chips - 1, 0, -1))
                yield far, times_listed(far_chip, core)
                yield lax.ppermute(far, "core", swap), times_listed(far_chip, other_core)
                return
            from_below = lax.ppermute(from_below, "chip", up)
            from_above = lax.ppermute(from_above, "chip", down)
            yield from_below, times_listed(chip - step, core)
            yield from_above, times_listed(chip + step, core)
            yield lax.ppermute(from_below, "core", swap), times_listed(chip - step, other_core)
            yield lax.ppermute(from_above, "core", swap), times_listed(chip + step, other_core)

    first, second = relay(halves[0]), relay(halves[1])
    for a, b in zip(first, second):
        acc = add_pair(acc, *a)
        acc = add_pair(acc, *b)
        acc = lax.optimization_barrier(acc)
    summed, squares = acc
    result = summed * lax.rsqrt(squares)[:, None] * live[:, None]
    result = result.astype(jnp.bfloat16).reshape(buckets, slot_rows, width)
    order = jnp.arange(buckets, dtype=jnp.int32) ^ bucket
    result = jnp.take(result, order, axis=0)
    return result.reshape(1, 1, rows, width)


def solution(mesh):
    devices = mesh.devices
    split = Mesh(
        devices.reshape(devices.shape[0], devices.shape[1] // CORES, CORES),
        ("bucket", "chip", "core"),
    )
    group = ("chip", "core")
    in_specs = (P("bucket", group, None, None, None), P("bucket", group, None, None))
    out_specs = P("bucket", group, None, None)
    return jax.shard_map(
        per_device, mesh=split, in_specs=in_specs, out_specs=out_specs, check_vma=False
    )
```

```python
import jax
import jax.numpy as jnp
from jax import lax
from jax.sharding import Mesh, PartitionSpec as P

ROUNDS = 4


EPS = 1e-06
TEMP = 12.0
CORES = 2
COUNT_ROWS = 16


def normalize(block):
    values = block.astype(jnp.float32)
    return (values * lax.rsqrt(jnp.sum(values * values, axis=-1, keepdims=True) + EPS)).astype(
        jnp.bfloat16
    )


def weigh(unit_a, unit_b, live_b, extra):
    scores = jnp.dot(unit_a, unit_b.T, preferred_element_type=jnp.float32)
    return jnp.exp(TEMP * scores) * live_b[None, :] * extra


def split_pieces(pieces, slot_rows):
    n, _, width = pieces.shape
    data = pieces[:, :slot_rows].reshape(n * slot_rows, width)
    piece_counts = pieces[:, slot_rows, 0].astype(jnp.int32)
    slot_index = lax.broadcasted_iota(jnp.int32, (n, slot_rows), 1)
    live = (slot_index < piece_counts[:, None]).astype(jnp.float32).reshape(-1)
    return data, live


def per_device(embeddings, counts):
    buckets = lax.axis_size("bucket")
    bucket = lax.axis_index("bucket")
    slot_rows = embeddings.shape[3]
    width = embeddings.shape[4]
    count_rows = jnp.zeros(embeddings.shape[2:3] + (COUNT_ROWS, width), jnp.bfloat16)
    count_rows = count_rows.at[:, 0, 0].set(counts[0, 0, :, 0].astype(jnp.bfloat16))
    packed = jnp.concatenate([embeddings[0, 0], count_rows], axis=1)

    arrived = [lax.dynamic_index_in_dim(packed, bucket, axis=0, keepdims=False)]
    for m in range(1, buckets):
        outgoing = lax.dynamic_index_in_dim(packed, bucket ^ m, axis=0, keepdims=False)
        arrived.append(lax.ppermute(outgoing, "bucket", [(i, i ^ m) for i in range(buckets)]))

    own_data, live = split_pieces(jnp.stack(arrived), slot_rows)
    rows = own_data.shape[0]
    chips = lax.axis_size("chip")
    cores = lax.axis_size("core")
    blocks = chips * cores
    chip = lax.axis_index("chip")
    core = lax.axis_index("core")
    position = chip * cores + core
    other_core = (core + 1) % cores

    unit = normalize(own_data)
    not_self = 1.0 - jnp.eye(rows, dtype=jnp.float32)
    own = weigh(unit, unit, live, not_self)
    summed = jnp.dot(own.astype(jnp.bfloat16), own_data, preferred_element_type=jnp.float32)
    squares = jnp.sum(own * own, axis=1)
    acc = (summed, squares)

    def times_listed(other_chip, other_core):
        block = other_chip * cores + other_core
        listed = jnp.int32(0)
        for dist in range(1, ROUNDS + 1):
            for sign in (1, -1):
                listed = listed + (((position + sign * dist) % blocks) == block).astype(jnp.int32)
        exists = (other_chip >= 0) & (other_chip < chips)
        return jnp.where(exists, listed, 0).astype(jnp.float32)

    def add_pair(acc, got, weight):
        summed, squares = acc
        got_data, got_live = split_pieces(got, slot_rows)
        weights = weigh(unit, normalize(got_data), got_live, 1.0)
        part = jnp.dot(weights.astype(jnp.bfloat16), got_data, preferred_element_type=jnp.float32)
        return (summed + weight * part, squares + weight * jnp.sum(weights * weights, axis=1))

    swap = [(c, (c + 1) % cores) for c in range(cores)]
    up = [(c, c + 1) for c in range(chips - 1)]
    down = [(c + 1, c) for c in range(chips - 1)]
    ends = chips >= 4

    def relay(piece):
        yield lax.ppermute(piece, "core", swap), times_listed(chip, other_core)
        from_below, from_above = piece, piece
        for step in range(1, chips):
            if ends and step + 1 == chips:
                outgoing = jnp.where(chip == chips - 2, from_below, from_above)
                far = lax.ppermute(outgoing, "chip", [(chips - 2, chips - 1), (1, 0)])
                far_chip = jnp.where(chip == 0, chips - 1, jnp.where(chip == chips - 1, 0, -1))
                yield far, times_listed(far_chip, core)
                yield lax.ppermute(far, "core", swap), times_listed(far_chip, other_core)
                return
            from_below = lax.ppermute(from_below, "chip", up)
            from_above = lax.ppermute(from_above, "chip", down)
            yield from_below, times_listed(chip - step, core)
            yield from_above, times_listed(chip + step, core)
            yield lax.ppermute(from_below, "core", swap), times_listed(chip - step, other_core)
            yield lax.ppermute(from_above, "core", swap), times_listed(chip + step, other_core)

    for got, weight in relay(jnp.stack(arrived)):
        acc = add_pair(acc, got, weight)
        acc = lax.optimization_barrier(acc)
    summed, squares = acc
    result = summed * lax.rsqrt(squares)[:, None] * live[:, None]
    result = result.astype(jnp.bfloat16).reshape(buckets, slot_rows, width)
    order = jnp.arange(buckets, dtype=jnp.int32) ^ bucket
    result = jnp.take(result, order, axis=0)
    return result.reshape(1, 1, rows, width)


def solution(mesh):
    devices = mesh.devices
    split = Mesh(
        devices.reshape(devices.shape[0], devices.shape[1] // CORES, CORES),
        ("bucket", "chip", "core"),
    )
    group = ("chip", "core")
    in_specs = (P("bucket", group, None, None, None), P("bucket", group, None, None))
    out_specs = P("bucket", group, None, None)
    return jax.shard_map(
        per_device, mesh=split, in_specs=in_specs, out_specs=out_specs, check_vma=False
    )
```

```python
import jax
import jax.numpy as jnp
from jax import lax
from jax.sharding import Mesh, PartitionSpec as P

ROUNDS = 4


EPS = 1e-06
TEMP = 12.0
CORES = 2


def normalize(block):
    values = block.astype(jnp.float32)
    return (values * lax.rsqrt(jnp.sum(values * values, axis=-1, keepdims=True) + EPS)).astype(
        jnp.bfloat16
    )


def weigh(unit_a, unit_b, live_b, extra):
    scores = jnp.dot(unit_a, unit_b.T, preferred_element_type=jnp.float32)
    return jnp.exp(TEMP * scores) * live_b[None, :] * extra


def live_of(block_counts, slot_rows):
    sources = block_counts.shape[0]
    slot_index = lax.broadcasted_iota(jnp.int32, (sources, slot_rows), 1)
    return (slot_index < block_counts.reshape(sources, 1)).astype(jnp.float32).reshape(-1)


def per_device(embeddings, counts):
    buckets = lax.axis_size("bucket")
    bucket = lax.axis_index("bucket")
    slot_rows = embeddings.shape[3]
    width = embeddings.shape[4]
    count_rows = jnp.zeros(embeddings.shape[2:3] + (16, width), jnp.bfloat16)
    count_rows = count_rows.at[:, 0, 0].set(counts[0, 0, :, 0].astype(jnp.bfloat16))
    packed = jnp.concatenate([embeddings[0, 0], count_rows], axis=1)
    arrived = [lax.dynamic_index_in_dim(packed, bucket, axis=0, keepdims=False)]
    for m in range(1, buckets):
        outgoing = lax.dynamic_index_in_dim(packed, bucket ^ m, axis=0, keepdims=False)
        arrived.append(lax.ppermute(outgoing, "bucket", [(i, i ^ m) for i in range(buckets)]))
    slabs = jnp.stack(arrived)
    sources = slabs.shape[0]
    rows = sources * slot_rows
    data = slabs[:, :slot_rows].reshape(rows, width)
    own_counts = slabs[:, slot_rows, 0].astype(jnp.int32)
    live = live_of(own_counts, slot_rows)
    chips = lax.axis_size("chip")
    cores = lax.axis_size("core")
    blocks = chips * cores
    chip = lax.axis_index("chip")
    core = lax.axis_index("core")
    position = chip * cores + core

    unit = normalize(data)
    not_self = 1.0 - jnp.eye(rows, dtype=jnp.float32)
    own = weigh(unit, unit, live, not_self)
    summed = jnp.dot(own.astype(jnp.bfloat16), data, preferred_element_type=jnp.float32)
    squares = jnp.sum(own * own, axis=1)

    def times_listed(other_chip, other_core):
        block = other_chip * cores + other_core
        listed = jnp.int32(0)
        for dist in range(1, ROUNDS + 1):
            for sign in (1, -1):
                listed = listed + (((position + sign * dist) % blocks) == block).astype(jnp.int32)
        exists = (other_chip >= 0) & (other_chip < chips)
        return jnp.where(exists, listed, 0).astype(jnp.float32)

    def pair_terms(acc, got, weight):
        summed, squares = acc
        got_data = got[:rows]
        got_counts = got[rows, :sources].astype(jnp.int32)
        weights = weigh(unit, normalize(got_data), live_of(got_counts, slot_rows), 1.0)
        part = jnp.dot(weights.astype(jnp.bfloat16), got_data, preferred_element_type=jnp.float32)
        return (summed + weight * part, squares + weight * jnp.sum(weights * weights, axis=1))

    def add_pair(acc, got, weight):
        return pair_terms(acc, got, weight)

    swap = [(c, (c + 1) % cores) for c in range(cores)]
    up = [(c, c + 1) for c in range(chips - 1)]
    down = [(c + 1, c) for c in range(chips - 1)]
    acc = (summed, squares)
    tail = jnp.zeros((16, width), jnp.bfloat16).at[0, :sources].set(own_counts.astype(jnp.bfloat16))
    mine = jnp.concatenate([data, tail], axis=0)
    other_core = (core + 1) % cores
    received = (lax.ppermute(mine, "chip", up), lax.ppermute(mine, "chip", down))
    swapped = lax.ppermute(mine, "core", swap)
    acc = add_pair(acc, swapped, times_listed(chip, other_core))
    for step in range(1, chips):
        acc, received = lax.optimization_barrier((acc, received))
        from_below, from_above = received
        if step + 2 < chips:
            received = (lax.ppermute(from_below, "chip", up), lax.ppermute(from_above, "chip", down))
        elif step + 2 == chips and chips >= 4:
            ends = [(chips - 2, chips - 1), (1, 0)]
            outgoing = jnp.where(chip == chips - 2, from_below, from_above)
            last = lax.ppermute(outgoing, "chip", ends)
            received = (last, last)
        elif step + 2 == chips:
            received = (lax.ppermute(from_below, "chip", up), lax.ppermute(from_above, "chip", down))
        if step + 1 == chips and chips >= 4:
            far_chip = jnp.where(chip == 0, chips - 1, jnp.where(chip == chips - 1, 0, -1))
            far_swapped = lax.ppermute(from_below, "core", swap)
            acc = add_pair(acc, from_below, times_listed(far_chip, core))
            acc = add_pair(acc, far_swapped, times_listed(far_chip, other_core))
            continue
        below_swapped = lax.ppermute(from_below, "core", swap)
        above_swapped = lax.ppermute(from_above, "core", swap)
        acc = add_pair(acc, from_below, times_listed(chip - step, core))
        acc = add_pair(acc, from_above, times_listed(chip + step, core))
        acc = add_pair(acc, below_swapped, times_listed(chip - step, other_core))
        acc = add_pair(acc, above_swapped, times_listed(chip + step, other_core))
    summed, squares = acc
    result = summed * lax.rsqrt(squares)[:, None] * live[:, None]
    result = result.astype(jnp.bfloat16).reshape(sources, slot_rows, width)
    order = jnp.arange(sources, dtype=jnp.int32) ^ bucket
    return jnp.take(result, order, axis=0).reshape(1, 1, rows, width)


def solution(mesh):
    devices = mesh.devices
    split = Mesh(
        devices.reshape(devices.shape[0], devices.shape[1] // CORES, CORES),
        ("bucket", "chip", "core"),
    )
    group = ("chip", "core")
    in_specs = (P("bucket", group, None, None, None), P("bucket", group, None, None))
    out_specs = P("bucket", group, None, None)
    return jax.shard_map(
        per_device, mesh=split, in_specs=in_specs, out_specs=out_specs, check_vma=False
    )
```

```python
import jax
import jax.numpy as jnp
from jax import lax
from jax.sharding import Mesh, PartitionSpec as P

ROUNDS = 4


EPS = 1e-06
TEMP = 12.0
CORES = 2


def normalize(block):
    values = block.astype(jnp.float32)
    return (values * lax.rsqrt(jnp.sum(values * values, axis=-1, keepdims=True) + EPS)).astype(
        jnp.bfloat16
    )


def weigh(unit_a, unit_b, live_b, extra):
    scores = jnp.dot(unit_a, unit_b.T, preferred_element_type=jnp.float32)
    return jnp.exp(TEMP * scores) * live_b[None, :] * extra


def live_of(block_counts, slot_rows):
    sources = block_counts.shape[0]
    slot_index = lax.broadcasted_iota(jnp.int32, (sources, slot_rows), 1)
    return (slot_index < block_counts.reshape(sources, 1)).astype(jnp.float32).reshape(-1)


def per_device(embeddings, counts):
    buckets = lax.axis_size("bucket")
    bucket = lax.axis_index("bucket")
    slot_rows = embeddings.shape[3]
    width = embeddings.shape[4]
    count_rows = jnp.zeros(embeddings.shape[2:3] + (16, width), jnp.bfloat16)
    count_rows = count_rows.at[:, 0, 0].set(counts[0, 0, :, 0].astype(jnp.bfloat16))
    packed = jnp.concatenate([embeddings[0, 0], count_rows], axis=1)
    arrived = [lax.dynamic_index_in_dim(packed, bucket, axis=0, keepdims=False)]
    for m in range(1, buckets):
        outgoing = lax.dynamic_index_in_dim(packed, bucket ^ m, axis=0, keepdims=False)
        arrived.append(lax.ppermute(outgoing, "bucket", [(i, i ^ m) for i in range(buckets)]))
    slabs = jnp.stack(arrived)
    sources = slabs.shape[0]
    rows = sources * slot_rows
    data = slabs[:, :slot_rows].reshape(rows, width)
    own_counts = slabs[:, slot_rows, 0].astype(jnp.int32)
    live = live_of(own_counts, slot_rows)
    chips = lax.axis_size("chip")
    cores = lax.axis_size("core")
    blocks = chips * cores
    chip = lax.axis_index("chip")
    core = lax.axis_index("core")
    position = chip * cores + core

    unit = normalize(data)
    not_self = 1.0 - jnp.eye(rows, dtype=jnp.float32)
    own = weigh(unit, unit, live, not_self)
    summed = jnp.dot(own.astype(jnp.bfloat16), data, preferred_element_type=jnp.float32)
    squares = jnp.sum(own * own, axis=1)

    def times_listed(other_chip, other_core):
        block = other_chip * cores + other_core
        listed = jnp.int32(0)
        for dist in range(1, ROUNDS + 1):
            for sign in (1, -1):
                listed = listed + (((position + sign * dist) % blocks) == block).astype(jnp.int32)
        exists = (other_chip >= 0) & (other_chip < chips)
        return jnp.where(exists, listed, 0).astype(jnp.float32)

    def pair_terms(acc, got, weight):
        summed, squares = acc
        got_data = got[:rows]
        got_counts = got[rows, :sources].astype(jnp.int32)
        weights = weigh(unit, normalize(got_data), live_of(got_counts, slot_rows), 1.0)
        part = jnp.dot(weights.astype(jnp.bfloat16), got_data, preferred_element_type=jnp.float32)
        return (summed + weight * part, squares + weight * jnp.sum(weights * weights, axis=1))

    def add_pair(acc, got, weight):
        return pair_terms(acc, got, weight)

    swap = [(c, (c + 1) % cores) for c in range(cores)]
    up = [(c, c + 1) for c in range(chips - 1)]
    down = [(c + 1, c) for c in range(chips - 1)]
    acc = (summed, squares)
    tail = jnp.zeros((16, width), jnp.bfloat16).at[0, :sources].set(own_counts.astype(jnp.bfloat16))
    mine = jnp.concatenate([data, tail], axis=0)
    other_core = (core + 1) % cores
    early = arrived[0]
    late_rows = jnp.concatenate([a[:slot_rows] for a in arrived[1:]], axis=0)
    late_tail = jnp.zeros((16, width), jnp.bfloat16).at[0, : sources - 1].set(
        own_counts[1:].astype(jnp.bfloat16)
    )
    late = jnp.concatenate([late_rows, late_tail], axis=0)

    def joined(first, rest):
        tail = jnp.zeros((16, width), jnp.bfloat16).at[0, 0].set(first[slot_rows, 0])
        tail = tail.at[0, 1:sources].set(rest[rows - slot_rows, : sources - 1])
        return jnp.concatenate([first[:slot_rows], rest[: rows - slot_rows], tail], axis=0)

    received = (
        joined(lax.ppermute(early, "chip", up), lax.ppermute(late, "chip", up)),
        joined(lax.ppermute(early, "chip", down), lax.ppermute(late, "chip", down)),
    )
    swapped = lax.ppermute(mine, "core", swap)
    acc = add_pair(acc, swapped, times_listed(chip, other_core))
    for step in range(1, chips):
        acc, received = lax.optimization_barrier((acc, received))
        from_below, from_above = received
        if step + 2 < chips:
            received = (lax.ppermute(from_below, "chip", up), lax.ppermute(from_above, "chip", down))
        elif step + 2 == chips and chips >= 4:
            ends = [(chips - 2, chips - 1), (1, 0)]
            outgoing = jnp.where(chip == chips - 2, from_below, from_above)
            last = lax.ppermute(outgoing, "chip", ends)
            received = (last, last)
        elif step + 2 == chips:
            received = (lax.ppermute(from_below, "chip", up), lax.ppermute(from_above, "chip", down))
        if step + 1 == chips and chips >= 4:
            far_chip = jnp.where(chip == 0, chips - 1, jnp.where(chip == chips - 1, 0, -1))
            far_swapped = lax.ppermute(from_below, "core", swap)
            acc = add_pair(acc, from_below, times_listed(far_chip, core))
            acc = add_pair(acc, far_swapped, times_listed(far_chip, other_core))
            continue
        below_swapped = lax.ppermute(from_below, "core", swap)
        above_swapped = lax.ppermute(from_above, "core", swap)
        acc = add_pair(acc, from_below, times_listed(chip - step, core))
        acc = add_pair(acc, from_above, times_listed(chip + step, core))
        acc = add_pair(acc, below_swapped, times_listed(chip - step, other_core))
        acc = add_pair(acc, above_swapped, times_listed(chip + step, other_core))
    summed, squares = acc
    result = summed * lax.rsqrt(squares)[:, None] * live[:, None]
    result = result.astype(jnp.bfloat16).reshape(sources, slot_rows, width)
    order = jnp.arange(sources, dtype=jnp.int32) ^ bucket
    return jnp.take(result, order, axis=0).reshape(1, 1, rows, width)


def solution(mesh):
    devices = mesh.devices
    split = Mesh(
        devices.reshape(devices.shape[0], devices.shape[1] // CORES, CORES),
        ("bucket", "chip", "core"),
    )
    group = ("chip", "core")
    in_specs = (P("bucket", group, None, None, None), P("bucket", group, None, None))
    out_specs = P("bucket", group, None, None)
    return jax.shard_map(
        per_device, mesh=split, in_specs=in_specs, out_specs=out_specs, check_vma=False
    )
```

```python
import jax
import jax.numpy as jnp
from jax import lax
from jax.sharding import Mesh, PartitionSpec as P

ROUNDS = 4


EPS = 1e-06
TEMP = 12.0
CORES = 2


def normalize(block):
    values = block.astype(jnp.float32)
    return (values * lax.rsqrt(jnp.sum(values * values, axis=-1, keepdims=True) + EPS)).astype(
        jnp.bfloat16
    )


def weigh(unit_a, unit_b, live_b, extra):
    scores = jnp.dot(unit_a, unit_b.T, preferred_element_type=jnp.float32)
    return jnp.exp(TEMP * scores) * live_b[None, :] * extra


def live_of(block_counts, slot_rows):
    sources = block_counts.shape[0]
    slot_index = lax.broadcasted_iota(jnp.int32, (sources, slot_rows), 1)
    return (slot_index < block_counts.reshape(sources, 1)).astype(jnp.float32).reshape(-1)


def per_device(embeddings, counts):
    buckets = lax.axis_size("bucket")
    bucket = lax.axis_index("bucket")
    slot_rows = embeddings.shape[3]
    width = embeddings.shape[4]
    count_rows = jnp.zeros(embeddings.shape[2:3] + (16, width), jnp.bfloat16)
    count_rows = count_rows.at[:, 0, 0].set(counts[0, 0, :, 0].astype(jnp.bfloat16))
    packed = jnp.concatenate([embeddings[0, 0], count_rows], axis=1)
    arrived = [lax.dynamic_index_in_dim(packed, bucket, axis=0, keepdims=False)]
    for m in range(1, buckets):
        outgoing = lax.dynamic_index_in_dim(packed, bucket ^ m, axis=0, keepdims=False)
        arrived.append(lax.ppermute(outgoing, "bucket", [(i, i ^ m) for i in range(buckets)]))
    slabs = jnp.stack(arrived)
    sources = slabs.shape[0]
    rows = sources * slot_rows
    data = slabs[:, :slot_rows].reshape(rows, width)
    own_counts = slabs[:, slot_rows, 0].astype(jnp.int32)
    live = live_of(own_counts, slot_rows)
    chips = lax.axis_size("chip")
    cores = lax.axis_size("core")
    blocks = chips * cores
    chip = lax.axis_index("chip")
    core = lax.axis_index("core")
    position = chip * cores + core

    unit = normalize(data)
    not_self = 1.0 - jnp.eye(rows, dtype=jnp.float32)
    own = weigh(unit, unit, live, not_self)
    summed = jnp.dot(own.astype(jnp.bfloat16), data, preferred_element_type=jnp.float32)
    squares = jnp.sum(own * own, axis=1)

    def times_listed(other_chip, other_core):
        block = other_chip * cores + other_core
        listed = jnp.int32(0)
        for dist in range(1, ROUNDS + 1):
            for sign in (1, -1):
                listed = listed + (((position + sign * dist) % blocks) == block).astype(jnp.int32)
        exists = (other_chip >= 0) & (other_chip < chips)
        return jnp.where(exists, listed, 0).astype(jnp.float32)

    def pair_terms(acc, got, weight):
        summed, squares = acc
        got_data = got[:, :slot_rows].reshape(-1, width)
        got_counts = got[:, slot_rows, 0].astype(jnp.int32)
        weights = weigh(unit, normalize(got_data), live_of(got_counts, slot_rows), 1.0)
        part = jnp.dot(weights.astype(jnp.bfloat16), got_data, preferred_element_type=jnp.float32)
        return (summed + weight * part, squares + weight * jnp.sum(weights * weights, axis=1))

    def add_pair(acc, got, weight):
        return pair_terms(acc, got, weight)

    acc = (summed, squares)
    half = sources // 2
    halves = [jnp.stack(arrived[:half]), jnp.stack(arrived[half:])]
    gathered = []
    for piece in halves:
        if gathered:
            piece, gathered[-1] = lax.optimization_barrier((piece, gathered[-1]))
        along = lax.all_gather(piece, "chip", axis=0, tiled=False)
        gathered.append(lax.all_gather(along, "core", axis=1, tiled=False))
    for index in range(len(gathered)):
        if index:
            acc, got_all = lax.optimization_barrier((acc, gathered[index]))
        else:
            got_all = gathered[index]
        for other_chip in range(chips):
            for other in range(cores):
                weight = times_listed(jnp.int32(other_chip), jnp.int32(other))
                acc = add_pair(acc, got_all[other_chip, other], weight)
                acc = lax.optimization_barrier(acc)
    summed, squares = acc
    result = summed * lax.rsqrt(squares)[:, None] * live[:, None]
    result = result.astype(jnp.bfloat16).reshape(sources, slot_rows, width)
    order = jnp.arange(sources, dtype=jnp.int32) ^ bucket
    return jnp.take(result, order, axis=0).reshape(1, 1, rows, width)


def solution(mesh):
    devices = mesh.devices
    split = Mesh(
        devices.reshape(devices.shape[0], devices.shape[1] // CORES, CORES),
        ("bucket", "chip", "core"),
    )
    group = ("chip", "core")
    in_specs = (P("bucket", group, None, None, None), P("bucket", group, None, None))
    out_specs = P("bucket", group, None, None)
    return jax.shard_map(
        per_device, mesh=split, in_specs=in_specs, out_specs=out_specs, check_vma=False
    )
```

```python
import jax
import jax.numpy as jnp
from jax import lax
from jax.sharding import Mesh, PartitionSpec as P

ROUNDS = 4


EPS = 1e-06
TEMP = 12.0
CORES = 2


def normalize(block):
    values = block.astype(jnp.float32)
    return (values * lax.rsqrt(jnp.sum(values * values, axis=-1, keepdims=True) + EPS)).astype(
        jnp.bfloat16
    )


def weigh(unit_a, unit_b, live_b, extra):
    scores = jnp.dot(unit_a, unit_b.T, preferred_element_type=jnp.float32)
    return jnp.exp(TEMP * scores) * live_b[None, :] * extra


def live_of(block_counts, slot_rows):
    sources = block_counts.shape[0]
    slot_index = lax.broadcasted_iota(jnp.int32, (sources, slot_rows), 1)
    return (slot_index < block_counts.reshape(sources, 1)).astype(jnp.float32).reshape(-1)


def per_device(embeddings, counts):
    buckets = lax.axis_size("bucket")
    bucket = lax.axis_index("bucket")
    slot_rows = embeddings.shape[3]
    width = embeddings.shape[4]
    count_rows = jnp.zeros(embeddings.shape[2:3] + (16, width), jnp.bfloat16)
    count_rows = count_rows.at[:, 0, 0].set(counts[0, 0, :, 0].astype(jnp.bfloat16))
    packed = jnp.concatenate([embeddings[0, 0], count_rows], axis=1)
    arrived = [lax.dynamic_index_in_dim(packed, bucket, axis=0, keepdims=False)]
    for m in range(1, buckets):
        outgoing = lax.dynamic_index_in_dim(packed, bucket ^ m, axis=0, keepdims=False)
        arrived.append(lax.ppermute(outgoing, "bucket", [(i, i ^ m) for i in range(buckets)]))
    slabs = jnp.stack(arrived)
    sources = slabs.shape[0]
    rows = sources * slot_rows
    data = slabs[:, :slot_rows].reshape(rows, width)
    own_counts = slabs[:, slot_rows, 0].astype(jnp.int32)
    live = live_of(own_counts, slot_rows)
    chips = lax.axis_size("chip")
    cores = lax.axis_size("core")
    blocks = chips * cores
    chip = lax.axis_index("chip")
    core = lax.axis_index("core")
    position = chip * cores + core

    unit = normalize(data)
    not_self = 1.0 - jnp.eye(rows, dtype=jnp.float32)
    own = weigh(unit, unit, live, not_self)
    summed = jnp.dot(own.astype(jnp.bfloat16), data, preferred_element_type=jnp.float32)
    squares = jnp.sum(own * own, axis=1)

    def times_listed(other_chip, other_core):
        block = other_chip * cores + other_core
        listed = jnp.int32(0)
        for dist in range(1, ROUNDS + 1):
            for sign in (1, -1):
                listed = listed + (((position + sign * dist) % blocks) == block).astype(jnp.int32)
        exists = (other_chip >= 0) & (other_chip < chips)
        return jnp.where(exists, listed, 0).astype(jnp.float32)

    def pair_terms(acc, got, weight):
        summed, squares = acc
        got_data = got[:rows]
        got_counts = got[rows, :sources].astype(jnp.int32)
        weights = weigh(unit, normalize(got_data), live_of(got_counts, slot_rows), 1.0)
        part = jnp.dot(weights.astype(jnp.bfloat16), got_data, preferred_element_type=jnp.float32)
        return (summed + weight * part, squares + weight * jnp.sum(weights * weights, axis=1))

    def add_pair(acc, got, weight):
        return pair_terms(acc, got, weight)

    swap = [(c, (c + 1) % cores) for c in range(cores)]
    up = [(c, c + 1) for c in range(chips - 1)]
    down = [(c + 1, c) for c in range(chips - 1)]
    acc = (summed, squares)
    tail = jnp.zeros((16, width), jnp.bfloat16).at[0, :sources].set(own_counts.astype(jnp.bfloat16))
    mine = jnp.concatenate([data, tail], axis=0)
    other_core = (core + 1) % cores
    received = (lax.ppermute(mine, "chip", up), lax.ppermute(mine, "chip", down))
    swapped = lax.ppermute(mine, "core", swap)
    acc = add_pair(acc, swapped, times_listed(chip, other_core))
    for step in range(1, chips):
        from_below, from_above = received
        if step + 2 < chips:
            received = (lax.ppermute(from_below, "chip", up), lax.ppermute(from_above, "chip", down))
        elif step + 2 == chips and chips >= 4:
            ends = [(chips - 2, chips - 1), (1, 0)]
            outgoing = jnp.where(chip == chips - 2, from_below, from_above)
            last = lax.ppermute(outgoing, "chip", ends)
            received = (last, last)
        elif step + 2 == chips:
            received = (lax.ppermute(from_below, "chip", up), lax.ppermute(from_above, "chip", down))
        if step + 1 == chips and chips >= 4:
            far_chip = jnp.where(chip == 0, chips - 1, jnp.where(chip == chips - 1, 0, -1))
            far_swapped = lax.ppermute(from_below, "core", swap)
            acc = add_pair(acc, from_below, times_listed(far_chip, core))
            acc = add_pair(acc, far_swapped, times_listed(far_chip, other_core))
            continue
        below_swapped = lax.ppermute(from_below, "core", swap)
        above_swapped = lax.ppermute(from_above, "core", swap)
        acc = add_pair(acc, from_below, times_listed(chip - step, core))
        acc = add_pair(acc, from_above, times_listed(chip + step, core))
        acc = add_pair(acc, below_swapped, times_listed(chip - step, other_core))
        acc = add_pair(acc, above_swapped, times_listed(chip + step, other_core))
    summed, squares = acc
    result = summed * lax.rsqrt(squares)[:, None] * live[:, None]
    result = result.astype(jnp.bfloat16).reshape(sources, slot_rows, width)
    order = jnp.arange(sources, dtype=jnp.int32) ^ bucket
    return jnp.take(result, order, axis=0).reshape(1, 1, rows, width)


def solution(mesh):
    devices = mesh.devices
    split = Mesh(
        devices.reshape(devices.shape[0], devices.shape[1] // CORES, CORES),
        ("bucket", "chip", "core"),
    )
    group = ("chip", "core")
    in_specs = (P("bucket", group, None, None, None), P("bucket", group, None, None))
    out_specs = P("bucket", group, None, None)
    return jax.shard_map(
        per_device, mesh=split, in_specs=in_specs, out_specs=out_specs, check_vma=False
    )
```

```python
import jax
import jax.numpy as jnp
from jax import lax
from jax.sharding import Mesh, PartitionSpec as P

ROUNDS = 4


EPS = 1e-06
TEMP = 12.0
DEAD = 1000.0
CORES = 2


def normalize(block):
    values = block.astype(jnp.float32)
    return (values * lax.rsqrt(jnp.sum(values * values, axis=-1, keepdims=True) + EPS)).astype(
        jnp.bfloat16
    )


def weigh(unit_a, unit_b, live_b, extra):
    scores = jnp.dot(unit_a, unit_b.T, preferred_element_type=jnp.float32)
    return jnp.exp(TEMP * scores) * live_b[None, :] * extra


def live_of(block):
    return (block[:, 0] < DEAD / 2).astype(jnp.float32)


def per_device(embeddings, counts):
    buckets = lax.axis_size("bucket")
    bucket = lax.axis_index("bucket")
    slot_rows = embeddings.shape[3]
    width = embeddings.shape[4]
    pieces = embeddings[0, 0]
    slot_index = lax.broadcasted_iota(jnp.int32, pieces.shape, 1)
    lane_index = lax.broadcasted_iota(jnp.int32, pieces.shape, 2)
    dead = (slot_index >= counts[0, 0, :, :, None]) & (lane_index == 0)
    marked = jnp.where(dead, jnp.bfloat16(DEAD), pieces)
    arrived = [lax.dynamic_index_in_dim(marked, bucket, axis=0, keepdims=False)]
    for m in range(1, buckets):
        outgoing = lax.dynamic_index_in_dim(marked, bucket ^ m, axis=0, keepdims=False)
        arrived.append(lax.ppermute(outgoing, "bucket", [(i, i ^ m) for i in range(buckets)]))
    sources = buckets
    rows = sources * slot_rows
    data = jnp.concatenate(arrived, axis=0)
    live = live_of(data)
    chips = lax.axis_size("chip")
    cores = lax.axis_size("core")
    blocks = chips * cores
    chip = lax.axis_index("chip")
    core = lax.axis_index("core")
    position = chip * cores + core

    unit = normalize(data)
    not_self = 1.0 - jnp.eye(rows, dtype=jnp.float32)
    own = weigh(unit, unit, live, not_self)
    summed = jnp.dot(own.astype(jnp.bfloat16), data, preferred_element_type=jnp.float32)
    squares = jnp.sum(own * own, axis=1)

    def times_listed(other_chip, other_core):
        block = other_chip * cores + other_core
        listed = jnp.int32(0)
        for dist in range(1, ROUNDS + 1):
            for sign in (1, -1):
                listed = listed + (((position + sign * dist) % blocks) == block).astype(jnp.int32)
        exists = (other_chip >= 0) & (other_chip < chips)
        return jnp.where(exists, listed, 0).astype(jnp.float32)

    def pair_terms(acc, got, weight):
        summed, squares = acc
        weights = weigh(unit, normalize(got), live_of(got), 1.0)
        part = jnp.dot(weights.astype(jnp.bfloat16), got, preferred_element_type=jnp.float32)
        return (summed + weight * part, squares + weight * jnp.sum(weights * weights, axis=1))

    def add_pair(acc, got, weight):
        return pair_terms(acc, got, weight)

    swap = [(c, (c + 1) % cores) for c in range(cores)]
    up = [(c, c + 1) for c in range(chips - 1)]
    down = [(c + 1, c) for c in range(chips - 1)]
    acc = (summed, squares)
    mine = data
    other_core = (core + 1) % cores
    received = (lax.ppermute(mine, "chip", up), lax.ppermute(mine, "chip", down))
    swapped = lax.ppermute(mine, "core", swap)
    acc = add_pair(acc, swapped, times_listed(chip, other_core))
    for step in range(1, chips):
        from_below, from_above = received
        if step + 2 < chips:
            received = (lax.ppermute(from_below, "chip", up), lax.ppermute(from_above, "chip", down))
        elif step + 2 == chips and chips >= 4:
            ends = [(chips - 2, chips - 1), (1, 0)]
            outgoing = jnp.where(chip == chips - 2, from_below, from_above)
            last = lax.ppermute(outgoing, "chip", ends)
            received = (last, last)
        elif step + 2 == chips:
            received = (lax.ppermute(from_below, "chip", up), lax.ppermute(from_above, "chip", down))
        if step + 1 == chips and chips >= 4:
            far_chip = jnp.where(chip == 0, chips - 1, jnp.where(chip == chips - 1, 0, -1))
            far_swapped = lax.ppermute(from_below, "core", swap)
            acc = add_pair(acc, from_below, times_listed(far_chip, core))
            acc = add_pair(acc, far_swapped, times_listed(far_chip, other_core))
            continue
        below_swapped = lax.ppermute(from_below, "core", swap)
        above_swapped = lax.ppermute(from_above, "core", swap)
        acc = add_pair(acc, from_below, times_listed(chip - step, core))
        acc = add_pair(acc, from_above, times_listed(chip + step, core))
        acc = add_pair(acc, below_swapped, times_listed(chip - step, other_core))
        acc = add_pair(acc, above_swapped, times_listed(chip + step, other_core))
    summed, squares = acc
    result = summed * lax.rsqrt(squares)[:, None] * live[:, None]
    result = result.astype(jnp.bfloat16).reshape(sources, slot_rows, width)
    order = jnp.arange(sources, dtype=jnp.int32) ^ bucket
    return jnp.take(result, order, axis=0).reshape(1, 1, rows, width)


def solution(mesh):
    devices = mesh.devices
    split = Mesh(
        devices.reshape(devices.shape[0], devices.shape[1] // CORES, CORES),
        ("bucket", "chip", "core"),
    )
    group = ("chip", "core")
    in_specs = (P("bucket", group, None, None, None), P("bucket", group, None, None))
    out_specs = P("bucket", group, None, None)
    return jax.shard_map(
        per_device, mesh=split, in_specs=in_specs, out_specs=out_specs, check_vma=False
    )
```

```python
import jax
import jax.numpy as jnp
from jax import lax
from jax.sharding import Mesh, PartitionSpec as P

ROUNDS = 4


EPS = 1e-06
TEMP = 12.0
DEAD = 1000.0
CORES = 2


def normalize(block):
    values = block.astype(jnp.float32)
    return (values * lax.rsqrt(jnp.sum(values * values, axis=-1, keepdims=True) + EPS)).astype(
        jnp.bfloat16
    )


def weigh(unit_a, unit_b, live_b, extra):
    scores = jnp.dot(unit_a, unit_b.T, preferred_element_type=jnp.float32)
    return jnp.exp(TEMP * scores) * live_b[None, :] * extra


def live_of(block):
    return (block[:, 0] < DEAD / 2).astype(jnp.float32)


def per_device(embeddings, counts):
    buckets = lax.axis_size("bucket")
    bucket = lax.axis_index("bucket")
    slot_rows = embeddings.shape[3]
    width = embeddings.shape[4]
    pieces = embeddings[0, 0]
    slot_index = lax.broadcasted_iota(jnp.int32, pieces.shape, 1)
    lane_index = lax.broadcasted_iota(jnp.int32, pieces.shape, 2)
    dead = (slot_index >= counts[0, 0, :, :, None]) & (lane_index == 0)
    marked = jnp.where(dead, jnp.bfloat16(DEAD), pieces)
    arrived = [lax.dynamic_index_in_dim(marked, bucket, axis=0, keepdims=False)]
    for m in range(1, buckets):
        outgoing = lax.dynamic_index_in_dim(marked, bucket ^ m, axis=0, keepdims=False)
        arrived.append(lax.ppermute(outgoing, "bucket", [(i, i ^ m) for i in range(buckets)]))
    sources = buckets
    rows = sources * slot_rows
    data = jnp.concatenate(arrived, axis=0)
    live = live_of(data)
    chips = lax.axis_size("chip")
    cores = lax.axis_size("core")
    blocks = chips * cores
    chip = lax.axis_index("chip")
    core = lax.axis_index("core")
    position = chip * cores + core

    unit = normalize(data)
    not_self = 1.0 - jnp.eye(rows, dtype=jnp.float32)
    own = weigh(unit, unit, live, not_self)
    summed = jnp.dot(own.astype(jnp.bfloat16), data, preferred_element_type=jnp.float32)
    squares = jnp.sum(own * own, axis=1)

    def times_listed(other_chip, other_core):
        block = other_chip * cores + other_core
        listed = jnp.int32(0)
        for dist in range(1, ROUNDS + 1):
            for sign in (1, -1):
                listed = listed + (((position + sign * dist) % blocks) == block).astype(jnp.int32)
        exists = (other_chip >= 0) & (other_chip < chips)
        return jnp.where(exists, listed, 0).astype(jnp.float32)

    def pair_terms(acc, got, weight):
        summed, squares = acc
        weights = weigh(unit, normalize(got), live_of(got), 1.0)
        part = jnp.dot(weights.astype(jnp.bfloat16), got, preferred_element_type=jnp.float32)
        return (summed + weight * part, squares + weight * jnp.sum(weights * weights, axis=1))

    def add_pair(acc, got, weight):
        return pair_terms(acc, got, weight)

    swap = [(c, (c + 1) % cores) for c in range(cores)]
    up = [(c, c + 1) for c in range(chips - 1)]
    down = [(c + 1, c) for c in range(chips - 1)]
    acc = (summed, squares)
    mine = data
    other_core = (core + 1) % cores
    received = (lax.ppermute(mine, "chip", up), lax.ppermute(mine, "chip", down))
    swapped = lax.ppermute(mine, "core", swap)
    acc = add_pair(acc, swapped, times_listed(chip, other_core))
    for step in range(1, chips):
        if step + 1 == chips:
            acc, received = lax.optimization_barrier((acc, received))
        from_below, from_above = received
        if step + 2 < chips:
            received = (lax.ppermute(from_below, "chip", up), lax.ppermute(from_above, "chip", down))
        elif step + 2 == chips and chips >= 4:
            ends = [(chips - 2, chips - 1), (1, 0)]
            outgoing = jnp.where(chip == chips - 2, from_below, from_above)
            last = lax.ppermute(outgoing, "chip", ends)
            received = (last, last)
        elif step + 2 == chips:
            received = (lax.ppermute(from_below, "chip", up), lax.ppermute(from_above, "chip", down))
        if step + 1 == chips and chips >= 4:
            far_chip = jnp.where(chip == 0, chips - 1, jnp.where(chip == chips - 1, 0, -1))
            far_swapped = lax.ppermute(from_below, "core", swap)
            acc = add_pair(acc, from_below, times_listed(far_chip, core))
            acc = add_pair(acc, far_swapped, times_listed(far_chip, other_core))
            continue
        below_swapped = lax.ppermute(from_below, "core", swap)
        above_swapped = lax.ppermute(from_above, "core", swap)
        acc = add_pair(acc, from_below, times_listed(chip - step, core))
        acc = add_pair(acc, from_above, times_listed(chip + step, core))
        acc = add_pair(acc, below_swapped, times_listed(chip - step, other_core))
        acc = add_pair(acc, above_swapped, times_listed(chip + step, other_core))
    summed, squares = acc
    result = summed * lax.rsqrt(squares)[:, None] * live[:, None]
    result = result.astype(jnp.bfloat16).reshape(sources, slot_rows, width)
    order = jnp.arange(sources, dtype=jnp.int32) ^ bucket
    return jnp.take(result, order, axis=0, mode="clip").reshape(1, 1, rows, width)


def solution(mesh):
    devices = mesh.devices
    split = Mesh(
        devices.reshape(devices.shape[0], devices.shape[1] // CORES, CORES),
        ("bucket", "chip", "core"),
    )
    group = ("chip", "core")
    in_specs = (P("bucket", group, None, None, None), P("bucket", group, None, None))
    out_specs = P("bucket", group, None, None)
    return jax.shard_map(
        per_device, mesh=split, in_specs=in_specs, out_specs=out_specs, check_vma=False
    )
```

```python
import jax
import jax.numpy as jnp
from jax import lax
from jax.sharding import Mesh, PartitionSpec as P

ROUNDS = 4


EPS = 1e-06
TEMP = 12.0
DEAD = 1000.0
CORES = 2


def normalize(block):
    values = block.astype(jnp.float32)
    return (values * lax.rsqrt(jnp.sum(values * values, axis=-1, keepdims=True) + EPS)).astype(
        jnp.bfloat16
    )


def weigh(unit_a, unit_b, live_b, extra):
    scores = jnp.dot(unit_a, unit_b.T, preferred_element_type=jnp.float32)
    return jnp.exp(TEMP * scores) * live_b[None, :] * extra


def live_of(block):
    return (block[:, 0] < DEAD / 2).astype(jnp.float32)


def per_device(embeddings, counts):
    buckets = lax.axis_size("bucket")
    bucket = lax.axis_index("bucket")
    slot_rows = embeddings.shape[3]
    width = embeddings.shape[4]
    pieces = embeddings[0, 0]
    slot_index = lax.broadcasted_iota(jnp.int32, pieces.shape, 1)
    lane_index = lax.broadcasted_iota(jnp.int32, pieces.shape, 2)
    dead = (slot_index >= counts[0, 0, :, :, None]) & (lane_index == 0)
    marked = jnp.where(dead, jnp.bfloat16(DEAD), pieces)
    arrived = [lax.dynamic_index_in_dim(marked, bucket, axis=0, keepdims=False)]
    for m in range(1, buckets):
        outgoing = lax.dynamic_index_in_dim(marked, bucket ^ m, axis=0, keepdims=False)
        arrived.append(lax.ppermute(outgoing, "bucket", [(i, i ^ m) for i in range(buckets)]))
    sources = buckets
    rows = sources * slot_rows
    data = jnp.zeros((rows, width), jnp.bfloat16)
    for m, piece in enumerate(arrived):
        data = lax.dynamic_update_slice_in_dim(data, piece, (bucket ^ m) * slot_rows, axis=0)
    live = live_of(data)
    chips = lax.axis_size("chip")
    cores = lax.axis_size("core")
    blocks = chips * cores
    chip = lax.axis_index("chip")
    core = lax.axis_index("core")
    position = chip * cores + core

    unit = normalize(data)
    not_self = 1.0 - jnp.eye(rows, dtype=jnp.float32)
    own = weigh(unit, unit, live, not_self)
    summed = jnp.dot(own.astype(jnp.bfloat16), data, preferred_element_type=jnp.float32)
    squares = jnp.sum(own * own, axis=1)

    def times_listed(other_chip, other_core):
        block = other_chip * cores + other_core
        listed = jnp.int32(0)
        for dist in range(1, ROUNDS + 1):
            for sign in (1, -1):
                listed = listed + (((position + sign * dist) % blocks) == block).astype(jnp.int32)
        exists = (other_chip >= 0) & (other_chip < chips)
        return jnp.where(exists, listed, 0).astype(jnp.float32)

    def pair_terms(acc, got, weight):
        summed, squares = acc
        weights = weigh(unit, normalize(got), live_of(got), 1.0)
        part = jnp.dot(weights.astype(jnp.bfloat16), got, preferred_element_type=jnp.float32)
        return (summed + weight * part, squares + weight * jnp.sum(weights * weights, axis=1))

    def add_pair(acc, got, weight):
        return pair_terms(acc, got, weight)

    swap = [(c, (c + 1) % cores) for c in range(cores)]
    up = [(c, c + 1) for c in range(chips - 1)]
    down = [(c + 1, c) for c in range(chips - 1)]
    acc = (summed, squares)
    mine = data
    other_core = (core + 1) % cores
    received = (lax.ppermute(mine, "chip", up), lax.ppermute(mine, "chip", down))
    swapped = lax.ppermute(mine, "core", swap)
    acc = add_pair(acc, swapped, times_listed(chip, other_core))
    for step in range(1, chips):
        if step + 1 == chips:
            acc, received = lax.optimization_barrier((acc, received))
        from_below, from_above = received
        if step + 2 < chips:
            received = (lax.ppermute(from_below, "chip", up), lax.ppermute(from_above, "chip", down))
        elif step + 2 == chips and chips >= 4:
            ends = [(chips - 2, chips - 1), (1, 0)]
            outgoing = jnp.where(chip == chips - 2, from_below, from_above)
            last = lax.ppermute(outgoing, "chip", ends)
            received = (last, last)
        elif step + 2 == chips:
            received = (lax.ppermute(from_below, "chip", up), lax.ppermute(from_above, "chip", down))
        if step + 1 == chips and chips >= 4:
            far_chip = jnp.where(chip == 0, chips - 1, jnp.where(chip == chips - 1, 0, -1))
            far_swapped = lax.ppermute(from_below, "core", swap)
            acc = add_pair(acc, from_below, times_listed(far_chip, core))
            acc = add_pair(acc, far_swapped, times_listed(far_chip, other_core))
            continue
        below_swapped = lax.ppermute(from_below, "core", swap)
        above_swapped = lax.ppermute(from_above, "core", swap)
        acc = add_pair(acc, from_below, times_listed(chip - step, core))
        acc = add_pair(acc, from_above, times_listed(chip + step, core))
        acc = add_pair(acc, below_swapped, times_listed(chip - step, other_core))
        acc = add_pair(acc, above_swapped, times_listed(chip + step, other_core))
    summed, squares = acc
    result = summed * lax.rsqrt(squares)[:, None] * live[:, None]
    return result.astype(jnp.bfloat16).reshape(1, 1, rows, width)


def solution(mesh):
    devices = mesh.devices
    split = Mesh(
        devices.reshape(devices.shape[0], devices.shape[1] // CORES, CORES),
        ("bucket", "chip", "core"),
    )
    group = ("chip", "core")
    in_specs = (P("bucket", group, None, None, None), P("bucket", group, None, None))
    out_specs = P("bucket", group, None, None)
    return jax.shard_map(
        per_device, mesh=split, in_specs=in_specs, out_specs=out_specs, check_vma=False
    )
```

```python
import jax
import jax.numpy as jnp
from jax import lax
from jax.sharding import Mesh, PartitionSpec as P

ROUNDS = 4


EPS = 1e-06
TEMP = 12.0
DEAD = 1000.0
CORES = 2


def normalize(block):
    values = block.astype(jnp.float32)
    return (values * lax.rsqrt(jnp.sum(values * values, axis=-1, keepdims=True) + EPS)).astype(
        jnp.bfloat16
    )


def weigh(unit_a, unit_b, live_b, extra):
    scores = jnp.dot(unit_a, unit_b.T, preferred_element_type=jnp.float32)
    return jnp.exp(TEMP * scores) * live_b[None, :] * extra


def live_of(block):
    return (block[:, 0] < DEAD / 2).astype(jnp.float32)


def per_device(embeddings, counts):
    buckets = lax.axis_size("bucket")
    bucket = lax.axis_index("bucket")
    slot_rows = embeddings.shape[3]
    width = embeddings.shape[4]
    pieces = embeddings[0, 0]
    slot_index = lax.broadcasted_iota(jnp.int32, pieces.shape, 1)
    lane_index = lax.broadcasted_iota(jnp.int32, pieces.shape, 2)
    dead = (slot_index >= counts[0, 0, :, :, None]) & (lane_index == 0)
    marked = jnp.where(dead, jnp.bfloat16(DEAD), pieces)
    arrived = [lax.dynamic_index_in_dim(marked, bucket, axis=0, keepdims=False)]
    for m in range(1, buckets):
        outgoing = lax.dynamic_index_in_dim(marked, bucket ^ m, axis=0, keepdims=False)
        arrived.append(lax.ppermute(outgoing, "bucket", [(i, i ^ m) for i in range(buckets)]))
    sources = buckets
    rows = sources * slot_rows
    data = jnp.zeros((rows, width), jnp.bfloat16)
    for m, piece in enumerate(arrived):
        data = lax.dynamic_update_slice_in_dim(data, piece, (bucket ^ m) * slot_rows, axis=0)
    live = live_of(data)
    chips = lax.axis_size("chip")
    cores = lax.axis_size("core")
    blocks = chips * cores
    chip = lax.axis_index("chip")
    core = lax.axis_index("core")
    position = chip * cores + core

    unit = normalize(data)
    not_self = 1.0 - jnp.eye(rows, dtype=jnp.float32)
    own = weigh(unit, unit, live, not_self)
    summed = jnp.dot(own.astype(jnp.bfloat16), data, preferred_element_type=jnp.float32)
    squares = jnp.sum(own * own, axis=1)

    def times_listed(other_chip, other_core):
        block = other_chip * cores + other_core
        listed = jnp.int32(0)
        for dist in range(1, ROUNDS + 1):
            for sign in (1, -1):
                listed = listed + (((position + sign * dist) % blocks) == block).astype(jnp.int32)
        exists = (other_chip >= 0) & (other_chip < chips)
        return jnp.where(exists, listed, 0).astype(jnp.float32)

    def pair_terms(acc, got, weight):
        summed, squares = acc
        weights = weigh(unit, normalize(got), live_of(got), 1.0)
        part = jnp.dot(weights.astype(jnp.bfloat16), got, preferred_element_type=jnp.float32)
        return (summed + weight * part, squares + weight * jnp.sum(weights * weights, axis=1))

    def add_pair(acc, got, weight):
        return pair_terms(acc, got, weight)

    swap = [(c, (c + 1) % cores) for c in range(cores)]
    exchange = [(z, z + 1) if z % 2 == 0 else (z, z - 1) for z in range(chips) if z % 2 or z + 1 < chips]
    across = [(z, z - 1) if z % 2 == 0 else (z, z + 1) for z in range(chips) if (z % 2 == 0 and z >= 2) or (z % 2 and z + 1 < chips)]
    upward = 1 - 2 * (chip % 2)
    acc = (summed, squares)
    mine = data
    other_core = (core + 1) % cores
    received = (lax.ppermute(mine, "chip", exchange), lax.ppermute(mine, "chip", across))
    swapped = lax.ppermute(mine, "core", swap)
    acc = add_pair(acc, swapped, times_listed(chip, other_core))
    for step in range(1, chips):
        if step + 1 == chips:
            acc, received = lax.optimization_barrier((acc, received))
        by_exchange, by_across = received
        if step + 2 < chips or (step + 2 == chips and chips < 4):
            received = (lax.ppermute(by_across, "chip", exchange), lax.ppermute(by_exchange, "chip", across))
        elif step + 2 == chips:
            last = lax.ppermute(by_across, "chip", [(chips - 2, chips - 1), (1, 0)])
            received = (last, last)
        if step + 1 == chips and chips >= 4:
            far_chip = jnp.where(chip == 0, chips - 1, jnp.where(chip == chips - 1, 0, -1))
            far = by_exchange
            far_swapped = lax.ppermute(far, "core", swap)
            acc = add_pair(acc, far, times_listed(far_chip, core))
            acc = add_pair(acc, far_swapped, times_listed(far_chip, other_core))
            continue
        exchange_chip = chip + upward * step
        across_chip = chip - upward * step
        exchange_swapped = lax.ppermute(by_exchange, "core", swap)
        across_swapped = lax.ppermute(by_across, "core", swap)
        acc = add_pair(acc, by_exchange, times_listed(exchange_chip, core))
        acc = add_pair(acc, by_across, times_listed(across_chip, core))
        acc = add_pair(acc, exchange_swapped, times_listed(exchange_chip, other_core))
        acc = add_pair(acc, across_swapped, times_listed(across_chip, other_core))
    summed, squares = acc
    result = summed * lax.rsqrt(squares)[:, None] * live[:, None]
    return result.astype(jnp.bfloat16).reshape(1, 1, rows, width)


def solution(mesh):
    devices = mesh.devices
    split = Mesh(
        devices.reshape(devices.shape[0], devices.shape[1] // CORES, CORES),
        ("bucket", "chip", "core"),
    )
    group = ("chip", "core")
    in_specs = (P("bucket", group, None, None, None), P("bucket", group, None, None))
    out_specs = P("bucket", group, None, None)
    return jax.shard_map(
        per_device, mesh=split, in_specs=in_specs, out_specs=out_specs, check_vma=False
    )
```

```python
import jax
import jax.numpy as jnp
from jax import lax
from jax.sharding import Mesh, PartitionSpec as P

ROUNDS = 4


EPS = 1e-06
TEMP = 12.0
DEAD = 1000.0
CORES = 2


def normalize(block):
    values = block.astype(jnp.float32)
    return (values * lax.rsqrt(jnp.sum(values * values, axis=-1, keepdims=True) + EPS)).astype(
        jnp.bfloat16
    )


def weigh(unit_a, unit_b, live_b, extra):
    scores = jnp.dot(unit_a, unit_b.T, preferred_element_type=jnp.float32)
    return jnp.exp(TEMP * scores) * live_b[None, :] * extra


def live_of(block):
    return (block[:, 0] < DEAD / 2).astype(jnp.float32)


def per_device(embeddings, counts):
    buckets = lax.axis_size("bucket")
    bucket = lax.axis_index("bucket")
    slot_rows = embeddings.shape[3]
    width = embeddings.shape[4]
    pieces = embeddings[0, 0]
    slot_index = lax.broadcasted_iota(jnp.int32, pieces.shape[1:], 0)
    lane_index = lax.broadcasted_iota(jnp.int32, pieces.shape[1:], 1)

    def marked(dest):
        piece = lax.dynamic_index_in_dim(pieces, dest, axis=0, keepdims=False)
        count = lax.dynamic_index_in_dim(counts[0, 0, :, 0], dest, axis=0, keepdims=False)
        return jnp.where((slot_index >= count) & (lane_index == 0), jnp.bfloat16(DEAD), piece)

    arrived = [marked(bucket)]
    for m in range(1, buckets):
        outgoing = marked(bucket ^ m)
        arrived.append(lax.ppermute(outgoing, "bucket", [(i, i ^ m) for i in range(buckets)]))
    sources = buckets
    rows = sources * slot_rows
    data = jnp.zeros((rows, width), jnp.bfloat16)
    for m, piece in enumerate(arrived):
        data = lax.dynamic_update_slice_in_dim(data, piece, (bucket ^ m) * slot_rows, axis=0)
    live = live_of(data)
    chips = lax.axis_size("chip")
    cores = lax.axis_size("core")
    blocks = chips * cores
    chip = lax.axis_index("chip")
    core = lax.axis_index("core")
    position = chip * cores + core

    unit = normalize(data)
    not_self = 1.0 - jnp.eye(rows, dtype=jnp.float32)
    own = weigh(unit, unit, live, not_self)
    summed = jnp.dot(own.astype(jnp.bfloat16), data, preferred_element_type=jnp.float32)
    squares = jnp.sum(own * own, axis=1)

    def times_listed(other_chip, other_core):
        block = other_chip * cores + other_core
        listed = jnp.int32(0)
        for dist in range(1, ROUNDS + 1):
            for sign in (1, -1):
                listed = listed + (((position + sign * dist) % blocks) == block).astype(jnp.int32)
        exists = (other_chip >= 0) & (other_chip < chips)
        return jnp.where(exists, listed, 0).astype(jnp.float32)

    def pair_terms(acc, got, weight):
        summed, squares = acc
        weights = weigh(unit, normalize(got), live_of(got), 1.0)
        part = jnp.dot(weights.astype(jnp.bfloat16), got, preferred_element_type=jnp.float32)
        return (summed + weight * part, squares + weight * jnp.sum(weights * weights, axis=1))

    def add_pair(acc, got, weight):
        return pair_terms(acc, got, weight)

    swap = [(c, (c + 1) % cores) for c in range(cores)]
    exchange = [(z, z + 1) if z % 2 == 0 else (z, z - 1) for z in range(chips) if z % 2 or z + 1 < chips]
    across = [(z, z - 1) if z % 2 == 0 else (z, z + 1) for z in range(chips) if (z % 2 == 0 and z >= 2) or (z % 2 and z + 1 < chips)]
    upward = 1 - 2 * (chip % 2)
    acc = (summed, squares)
    mine = data
    other_core = (core + 1) % cores
    received = (lax.ppermute(mine, "chip", exchange), lax.ppermute(mine, "chip", across))
    swapped = lax.ppermute(mine, "core", swap)
    acc = add_pair(acc, swapped, times_listed(chip, other_core))
    for step in range(1, chips):
        if step + 1 == chips:
            acc, received = lax.optimization_barrier((acc, received))
        by_exchange, by_across = received
        if step + 2 < chips or (step + 2 == chips and chips < 4):
            received = (lax.ppermute(by_across, "chip", exchange), lax.ppermute(by_exchange, "chip", across))
        elif step + 2 == chips:
            last = lax.ppermute(by_across, "chip", [(chips - 2, chips - 1), (1, 0)])
            received = (last, last)
        if step + 1 == chips and chips >= 4:
            far_chip = jnp.where(chip == 0, chips - 1, jnp.where(chip == chips - 1, 0, -1))
            far = by_exchange
            far_swapped = lax.ppermute(far, "core", swap)
            acc = add_pair(acc, far, times_listed(far_chip, core))
            acc = add_pair(acc, far_swapped, times_listed(far_chip, other_core))
            continue
        exchange_chip = chip + upward * step
        across_chip = chip - upward * step
        exchange_swapped = lax.ppermute(by_exchange, "core", swap)
        across_swapped = lax.ppermute(by_across, "core", swap)
        acc = add_pair(acc, by_exchange, times_listed(exchange_chip, core))
        acc = add_pair(acc, by_across, times_listed(across_chip, core))
        acc = add_pair(acc, exchange_swapped, times_listed(exchange_chip, other_core))
        acc = add_pair(acc, across_swapped, times_listed(across_chip, other_core))
    summed, squares = acc
    result = summed * lax.rsqrt(squares)[:, None] * live[:, None]
    return result.astype(jnp.bfloat16).reshape(1, 1, rows, width)


def solution(mesh):
    devices = mesh.devices
    split = Mesh(
        devices.reshape(devices.shape[0], devices.shape[1] // CORES, CORES),
        ("bucket", "chip", "core"),
    )
    group = ("chip", "core")
    in_specs = (P("bucket", group, None, None, None), P("bucket", group, None, None))
    out_specs = P("bucket", group, None, None)
    return jax.shard_map(
        per_device, mesh=split, in_specs=in_specs, out_specs=out_specs, check_vma=False
    )
```

```python
import jax
import jax.numpy as jnp
from jax import lax
from jax.sharding import Mesh, PartitionSpec as P

ROUNDS = 4


EPS = 1e-06
TEMP = 12.0
DEAD = 1000.0
CORES = 2


def normalize(block):
    values = block.astype(jnp.float32)
    return (values * lax.rsqrt(jnp.sum(values * values, axis=-1, keepdims=True) + EPS)).astype(
        jnp.bfloat16
    )


def weigh(unit_a, unit_b, live_b, extra):
    scores = jnp.dot(unit_a, unit_b.T, preferred_element_type=jnp.float32)
    return jnp.exp(TEMP * scores) * live_b[None, :] * extra


def live_of(block):
    return (block[:, 0] < DEAD / 2).astype(jnp.float32)


def per_device(embeddings, counts):
    buckets = lax.axis_size("bucket")
    bucket = lax.axis_index("bucket")
    slot_rows = embeddings.shape[3]
    width = embeddings.shape[4]
    pieces = embeddings[0, 0]
    slot_index = lax.broadcasted_iota(jnp.int32, pieces.shape, 1)
    lane_index = lax.broadcasted_iota(jnp.int32, pieces.shape, 2)
    dead = (slot_index >= counts[0, 0, :, :, None]) & (lane_index == 0)
    marked = jnp.where(dead, jnp.bfloat16(DEAD), pieces)
    arrived = [lax.dynamic_index_in_dim(marked, bucket, axis=0, keepdims=False)]
    for m in range(1, buckets):
        outgoing = lax.dynamic_index_in_dim(marked, bucket ^ m, axis=0, keepdims=False)
        arrived.append(lax.ppermute(outgoing, "bucket", [(i, i ^ m) for i in range(buckets)]))
    sources = buckets
    rows = sources * slot_rows
    data = jnp.zeros((rows, width), jnp.bfloat16)
    for m, piece in enumerate(arrived):
        data = lax.dynamic_update_slice_in_dim(data, piece, (bucket ^ m) * slot_rows, axis=0)
    live = live_of(data)
    chips = lax.axis_size("chip")
    cores = lax.axis_size("core")
    blocks = chips * cores
    chip = lax.axis_index("chip")
    core = lax.axis_index("core")
    position = chip * cores + core

    unit = normalize(data)
    not_self = 1.0 - jnp.eye(rows, dtype=jnp.float32)
    own = weigh(unit, unit, live, not_self)
    summed = jnp.dot(own.astype(jnp.bfloat16), data, preferred_element_type=jnp.float32)
    squares = jnp.sum(own * own, axis=1)

    def times_listed(other_chip, other_core):
        block = other_chip * cores + other_core
        listed = jnp.int32(0)
        for dist in range(1, ROUNDS + 1):
            for sign in (1, -1):
                listed = listed + (((position + sign * dist) % blocks) == block).astype(jnp.int32)
        exists = (other_chip >= 0) & (other_chip < chips)
        return jnp.where(exists, listed, 0).astype(jnp.float32)

    def pair_terms(acc, got, weight):
        summed, squares = acc
        weights = weigh(unit, normalize(got), live_of(got), 1.0)
        part = jnp.dot(weights.astype(jnp.bfloat16), got, preferred_element_type=jnp.float32)
        return (summed + weight * part, squares + weight * jnp.sum(weights * weights, axis=1))

    def add_pair(acc, got, weight):
        return pair_terms(acc, got, weight)

    swap = [(c, (c + 1) % cores) for c in range(cores)]
    exchange = [(z, z + 1) if z % 2 == 0 else (z, z - 1) for z in range(chips) if z % 2 or z + 1 < chips]
    across = [(z, z - 1) if z % 2 == 0 else (z, z + 1) for z in range(chips) if (z % 2 == 0 and z >= 2) or (z % 2 and z + 1 < chips)]
    upward = 1 - 2 * (chip % 2)
    acc = (summed, squares)
    mine = data
    other_core = (core + 1) % cores
    received = (lax.ppermute(mine, "chip", exchange), lax.ppermute(mine, "chip", across))
    swapped = lax.ppermute(mine, "core", swap)
    acc = add_pair(acc, swapped, times_listed(chip, other_core))
    for step in range(1, chips):
        if step > 1:
            acc, received = lax.optimization_barrier((acc, received))
        by_exchange, by_across = received
        if step + 2 < chips or (step + 2 == chips and chips < 4):
            received = (lax.ppermute(by_across, "chip", exchange), lax.ppermute(by_exchange, "chip", across))
        elif step + 2 == chips:
            last = lax.ppermute(by_across, "chip", [(chips - 2, chips - 1), (1, 0)])
            received = (last, last)
        if step + 1 == chips and chips >= 4:
            far_chip = jnp.where(chip == 0, chips - 1, jnp.where(chip == chips - 1, 0, -1))
            far = by_exchange
            far_swapped = lax.ppermute(far, "core", swap)
            acc = add_pair(acc, far, times_listed(far_chip, core))
            acc = add_pair(acc, far_swapped, times_listed(far_chip, other_core))
            continue
        exchange_chip = chip + upward * step
        across_chip = chip - upward * step
        exchange_swapped = lax.ppermute(by_exchange, "core", swap)
        across_swapped = lax.ppermute(by_across, "core", swap)
        acc = add_pair(acc, by_exchange, times_listed(exchange_chip, core))
        acc = add_pair(acc, by_across, times_listed(across_chip, core))
        acc = add_pair(acc, exchange_swapped, times_listed(exchange_chip, other_core))
        acc = add_pair(acc, across_swapped, times_listed(across_chip, other_core))
    summed, squares = acc
    result = summed * lax.rsqrt(squares)[:, None] * live[:, None]
    return result.astype(jnp.bfloat16).reshape(1, 1, rows, width)


def solution(mesh):
    devices = mesh.devices
    split = Mesh(
        devices.reshape(devices.shape[0], devices.shape[1] // CORES, CORES),
        ("bucket", "chip", "core"),
    )
    group = ("chip", "core")
    in_specs = (P("bucket", group, None, None, None), P("bucket", group, None, None))
    out_specs = P("bucket", group, None, None)
    return jax.shard_map(
        per_device, mesh=split, in_specs=in_specs, out_specs=out_specs, check_vma=False
    )
```

```python
import jax
import jax.numpy as jnp
from jax import lax
from jax.sharding import Mesh, PartitionSpec as P

ROUNDS = 4


EPS = 1e-06
TEMP = 12.0
DEAD = 1000.0
CORES = 2


def normalize(block):
    values = block.astype(jnp.float32)
    return (values * lax.rsqrt(jnp.sum(values * values, axis=-1, keepdims=True) + EPS)).astype(
        jnp.bfloat16
    )


def weigh(unit_a, unit_b, live_b, extra):
    scores = jnp.dot(unit_a, unit_b.T, preferred_element_type=jnp.float32)
    return jnp.exp(TEMP * scores) * live_b[None, :] * extra


def live_of(block):
    return (block[:, 0] < DEAD / 2).astype(jnp.float32)


def per_device(embeddings, counts):
    buckets = lax.axis_size("bucket")
    bucket = lax.axis_index("bucket")
    slot_rows = embeddings.shape[3]
    width = embeddings.shape[4]
    pieces = embeddings[0, 0]
    slot_index = lax.broadcasted_iota(jnp.int32, pieces.shape, 1)
    lane_index = lax.broadcasted_iota(jnp.int32, pieces.shape, 2)
    dead = (slot_index >= counts[0, 0, :, :, None]) & (lane_index == 0)
    marked = jnp.where(dead, jnp.bfloat16(DEAD), pieces)
    arrived = [lax.dynamic_index_in_dim(marked, bucket, axis=0, keepdims=False)]
    for m in range(1, buckets):
        outgoing = lax.dynamic_index_in_dim(marked, bucket ^ m, axis=0, keepdims=False)
        arrived.append(lax.ppermute(outgoing, "bucket", [(i, i ^ m) for i in range(buckets)]))
    sources = buckets
    rows = sources * slot_rows
    data = jnp.zeros((rows, width), jnp.bfloat16)
    for m, piece in enumerate(arrived):
        data = lax.dynamic_update_slice_in_dim(data, piece, (bucket ^ m) * slot_rows, axis=0)
    live = live_of(data)
    chips = lax.axis_size("chip")
    cores = lax.axis_size("core")
    blocks = chips * cores
    chip = lax.axis_index("chip")
    core = lax.axis_index("core")
    position = chip * cores + core

    unit = normalize(data)
    not_self = 1.0 - jnp.eye(rows, dtype=jnp.float32)
    own = weigh(unit, unit, live, not_self)
    summed = jnp.dot(own.astype(jnp.bfloat16), data, preferred_element_type=jnp.float32)
    squares = jnp.sum(own * own, axis=1)

    def times_listed(other_chip, other_core):
        block = other_chip * cores + other_core
        listed = jnp.int32(0)
        for dist in range(1, ROUNDS + 1):
            for sign in (1, -1):
                listed = listed + (((position + sign * dist) % blocks) == block).astype(jnp.int32)
        exists = (other_chip >= 0) & (other_chip < chips)
        return jnp.where(exists, listed, 0).astype(jnp.float32)

    def pair_terms(acc, got, weight):
        summed, squares = acc
        weights = weigh(unit, normalize(got), live_of(got), 1.0)
        part = jnp.dot(weights.astype(jnp.bfloat16), got, preferred_element_type=jnp.float32)
        return (summed + weight * part, squares + weight * jnp.sum(weights * weights, axis=1))

    def add_pair(acc, got, weight):
        return pair_terms(acc, got, weight)

    swap = [(c, (c + 1) % cores) for c in range(cores)]
    exchange = [(z, z + 1) if z % 2 == 0 else (z, z - 1) for z in range(chips) if z % 2 or z + 1 < chips]
    across = [(z, z - 1) if z % 2 == 0 else (z, z + 1) for z in range(chips) if (z % 2 == 0 and z >= 2) or (z % 2 and z + 1 < chips)]
    upward = 1 - 2 * (chip % 2)
    acc = (summed, squares)
    mine = data
    other_core = (core + 1) % cores
    received = (lax.ppermute(mine, "chip", exchange), lax.ppermute(mine, "chip", across))
    swapped = lax.ppermute(mine, "core", swap)
    acc = add_pair(acc, swapped, times_listed(chip, other_core))
    for step in range(1, chips):
        if step + 1 == chips:
            acc, received = lax.optimization_barrier((acc, received))
        by_exchange, by_across = received
        if step + 2 < chips or (step + 2 == chips and chips < 4):
            received = (lax.ppermute(by_across, "chip", exchange), lax.ppermute(by_exchange, "chip", across))
        elif step + 2 == chips:
            ends = [(chips - 2, chips - 1), (1, 0)]
            half = rows // 2
            received = (
                lax.ppermute(by_across[:half], "chip", ends),
                lax.ppermute(by_across[half:], "chip", ends),
            )
        if step + 1 == chips and chips >= 4:
            far_chip = jnp.where(chip == 0, chips - 1, jnp.where(chip == chips - 1, 0, -1))
            for far in received:
                far_swapped = lax.ppermute(far, "core", swap)
                acc = add_pair(acc, far, times_listed(far_chip, core))
                acc = add_pair(acc, far_swapped, times_listed(far_chip, other_core))
            continue
        exchange_chip = chip + upward * step
        across_chip = chip - upward * step
        exchange_swapped = lax.ppermute(by_exchange, "core", swap)
        across_swapped = lax.ppermute(by_across, "core", swap)
        acc = add_pair(acc, by_exchange, times_listed(exchange_chip, core))
        acc = add_pair(acc, by_across, times_listed(across_chip, core))
        acc = add_pair(acc, exchange_swapped, times_listed(exchange_chip, other_core))
        acc = add_pair(acc, across_swapped, times_listed(across_chip, other_core))
    summed, squares = acc
    result = summed * lax.rsqrt(squares)[:, None] * live[:, None]
    return result.astype(jnp.bfloat16).reshape(1, 1, rows, width)


def solution(mesh):
    devices = mesh.devices
    split = Mesh(
        devices.reshape(devices.shape[0], devices.shape[1] // CORES, CORES),
        ("bucket", "chip", "core"),
    )
    group = ("chip", "core")
    in_specs = (P("bucket", group, None, None, None), P("bucket", group, None, None))
    out_specs = P("bucket", group, None, None)
    return jax.shard_map(
        per_device, mesh=split, in_specs=in_specs, out_specs=out_specs, check_vma=False
    )
```

```python
import jax
import jax.numpy as jnp
from jax import lax
from jax.sharding import Mesh, PartitionSpec as P

ROUNDS = 4


EPS = 1e-06
TEMP = 12.0
DEAD = 1000.0
CORES = 2


def normalize(block):
    values = block.astype(jnp.float32)
    return (values * lax.rsqrt(jnp.sum(values * values, axis=-1, keepdims=True) + EPS)).astype(
        jnp.bfloat16
    )


def weigh(unit_a, unit_b, live_b, extra):
    scores = jnp.dot(unit_a, unit_b.T, preferred_element_type=jnp.float32)
    return jnp.exp(TEMP * scores) * live_b[None, :] * extra


def live_of(block):
    return (block[:, 0] < DEAD / 2).astype(jnp.float32)


def per_device(embeddings, counts):
    buckets = lax.axis_size("bucket")
    bucket = lax.axis_index("bucket")
    slot_rows = embeddings.shape[3]
    width = embeddings.shape[4]
    pieces = embeddings[0, 0]
    slot_index = lax.broadcasted_iota(jnp.int32, pieces.shape, 1)
    lane_index = lax.broadcasted_iota(jnp.int32, pieces.shape, 2)
    dead = (slot_index >= counts[0, 0, :, :, None]) & (lane_index == 0)
    marked = jnp.where(dead, jnp.bfloat16(DEAD), pieces)
    arrived = [lax.dynamic_index_in_dim(marked, bucket, axis=0, keepdims=False)]
    for m in range(1, buckets):
        outgoing = lax.dynamic_index_in_dim(marked, bucket ^ m, axis=0, keepdims=False)
        arrived.append(lax.ppermute(outgoing, "bucket", [(i, i ^ m) for i in range(buckets)]))
    sources = buckets
    rows = sources * slot_rows
    data = jnp.zeros((rows, width), jnp.bfloat16)
    for m, piece in enumerate(arrived):
        data = lax.dynamic_update_slice_in_dim(data, piece, (bucket ^ m) * slot_rows, axis=0)
    live = live_of(data)
    chips = lax.axis_size("chip")
    cores = lax.axis_size("core")
    blocks = chips * cores
    chip = lax.axis_index("chip")
    core = lax.axis_index("core")
    position = chip * cores + core

    unit = normalize(data)
    not_self = 1.0 - jnp.eye(rows, dtype=jnp.float32)
    own = weigh(unit, unit, live, not_self)
    summed = jnp.dot(own.astype(jnp.bfloat16), data, preferred_element_type=jnp.float32)
    squares = jnp.sum(own * own, axis=1)

    def times_listed(other_chip, other_core):
        block = other_chip * cores + other_core
        listed = jnp.int32(0)
        for dist in range(1, ROUNDS + 1):
            for sign in (1, -1):
                listed = listed + (((position + sign * dist) % blocks) == block).astype(jnp.int32)
        exists = (other_chip >= 0) & (other_chip < chips)
        return jnp.where(exists, listed, 0).astype(jnp.float32)

    def pair_terms(acc, got, weight):
        summed, squares = acc
        weights = weigh(unit, normalize(got), live_of(got), 1.0)
        part = jnp.dot(weights.astype(jnp.bfloat16), got, preferred_element_type=jnp.float32)
        return (summed + weight * part, squares + weight * jnp.sum(weights * weights, axis=1))

    def add_pair(acc, got, weight):
        return pair_terms(acc, got, weight)

    swap = [(c, (c + 1) % cores) for c in range(cores)]
    exchange = [(z, z + 1) if z % 2 == 0 else (z, z - 1) for z in range(chips) if z % 2 or z + 1 < chips]
    across = [(z, z - 1) if z % 2 == 0 else (z, z + 1) for z in range(chips) if (z % 2 == 0 and z >= 2) or (z % 2 and z + 1 < chips)]
    upward = 1 - 2 * (chip % 2)
    acc = (summed, squares)
    half = rows // 2
    mine = (data[:half], data[half:])
    other_core = (core + 1) % cores

    def send(parts, pairs):
        return tuple(lax.ppermute(part, "chip", pairs) for part in parts)

    def add_all(acc, parts, weight):
        for part in parts:
            acc = add_pair(acc, part, weight)
        return lax.optimization_barrier(acc)

    def swapped(parts):
        return tuple(lax.ppermute(part, "core", swap) for part in parts)

    received = (send(mine, exchange), send(mine, across))
    acc = add_all(acc, swapped(mine), times_listed(chip, other_core))
    for step in range(1, chips):
        if step + 1 == chips:
            acc, received = lax.optimization_barrier((acc, received))
        by_exchange, by_across = received
        if step + 2 < chips or (step + 2 == chips and chips < 4):
            received = (send(by_across, exchange), send(by_exchange, across))
        elif step + 2 == chips:
            far = send(by_across, [(chips - 2, chips - 1), (1, 0)])
            received = (far, far)
        if step + 1 == chips and chips >= 4:
            far_chip = jnp.where(chip == 0, chips - 1, jnp.where(chip == chips - 1, 0, -1))
            acc = add_all(acc, by_exchange, times_listed(far_chip, core))
            acc = add_all(acc, swapped(by_exchange), times_listed(far_chip, other_core))
            continue
        exchange_chip = chip + upward * step
        across_chip = chip - upward * step
        exchange_swapped = swapped(by_exchange)
        across_swapped = swapped(by_across)
        acc = add_all(acc, by_exchange, times_listed(exchange_chip, core))
        acc = add_all(acc, by_across, times_listed(across_chip, core))
        acc = add_all(acc, exchange_swapped, times_listed(exchange_chip, other_core))
        acc = add_all(acc, across_swapped, times_listed(across_chip, other_core))
    summed, squares = acc
    result = summed * lax.rsqrt(squares)[:, None] * live[:, None]
    return result.astype(jnp.bfloat16).reshape(1, 1, rows, width)


def solution(mesh):
    devices = mesh.devices
    split = Mesh(
        devices.reshape(devices.shape[0], devices.shape[1] // CORES, CORES),
        ("bucket", "chip", "core"),
    )
    group = ("chip", "core")
    in_specs = (P("bucket", group, None, None, None), P("bucket", group, None, None))
    out_specs = P("bucket", group, None, None)
    return jax.shard_map(
        per_device, mesh=split, in_specs=in_specs, out_specs=out_specs, check_vma=False
    )
```

```python
import jax
import jax.numpy as jnp
from jax import lax
from jax.sharding import Mesh, PartitionSpec as P

ROUNDS = 4


EPS = 1e-06
TEMP = 12.0
DEAD = 1000.0
CORES = 2
LAST_PARTS = 4


def normalize(block):
    values = block.astype(jnp.float32)
    return (values * lax.rsqrt(jnp.sum(values * values, axis=-1, keepdims=True) + EPS)).astype(
        jnp.bfloat16
    )


def weigh(unit_a, unit_b, live_b, extra):
    scores = jnp.dot(unit_a, unit_b.T, preferred_element_type=jnp.float32)
    return jnp.exp(TEMP * scores) * live_b[None, :] * extra


def live_of(block):
    return (block[:, 0] < DEAD / 2).astype(jnp.float32)


def per_device(embeddings, counts):
    buckets = lax.axis_size("bucket")
    bucket = lax.axis_index("bucket")
    slot_rows = embeddings.shape[3]
    width = embeddings.shape[4]
    pieces = embeddings[0, 0]
    slot_index = lax.broadcasted_iota(jnp.int32, pieces.shape, 1)
    lane_index = lax.broadcasted_iota(jnp.int32, pieces.shape, 2)
    dead = (slot_index >= counts[0, 0, :, :, None]) & (lane_index == 0)
    marked = jnp.where(dead, jnp.bfloat16(DEAD), pieces)
    arrived = [lax.dynamic_index_in_dim(marked, bucket, axis=0, keepdims=False)]
    for m in range(1, buckets):
        outgoing = lax.dynamic_index_in_dim(marked, bucket ^ m, axis=0, keepdims=False)
        arrived.append(lax.ppermute(outgoing, "bucket", [(i, i ^ m) for i in range(buckets)]))
    sources = buckets
    rows = sources * slot_rows
    data = jnp.zeros((rows, width), jnp.bfloat16)
    for m, piece in enumerate(arrived):
        data = lax.dynamic_update_slice_in_dim(data, piece, (bucket ^ m) * slot_rows, axis=0)
    live = live_of(data)
    chips = lax.axis_size("chip")
    cores = lax.axis_size("core")
    blocks = chips * cores
    chip = lax.axis_index("chip")
    core = lax.axis_index("core")
    position = chip * cores + core

    unit = normalize(data)
    not_self = 1.0 - jnp.eye(rows, dtype=jnp.float32)
    own = weigh(unit, unit, live, not_self)
    summed = jnp.dot(own.astype(jnp.bfloat16), data, preferred_element_type=jnp.float32)
    squares = jnp.sum(own * own, axis=1)

    def times_listed(other_chip, other_core):
        block = other_chip * cores + other_core
        listed = jnp.int32(0)
        for dist in range(1, ROUNDS + 1):
            for sign in (1, -1):
                listed = listed + (((position + sign * dist) % blocks) == block).astype(jnp.int32)
        exists = (other_chip >= 0) & (other_chip < chips)
        return jnp.where(exists, listed, 0).astype(jnp.float32)

    def pair_terms(acc, got, weight):
        summed, squares = acc
        weights = weigh(unit, normalize(got), live_of(got), 1.0)
        part = jnp.dot(weights.astype(jnp.bfloat16), got, preferred_element_type=jnp.float32)
        return (summed + weight * part, squares + weight * jnp.sum(weights * weights, axis=1))

    def add_pair(acc, got, weight):
        return pair_terms(acc, got, weight)

    swap = [(c, (c + 1) % cores) for c in range(cores)]
    exchange = [(z, z + 1) if z % 2 == 0 else (z, z - 1) for z in range(chips) if z % 2 or z + 1 < chips]
    across = [(z, z - 1) if z % 2 == 0 else (z, z + 1) for z in range(chips) if (z % 2 == 0 and z >= 2) or (z % 2 and z + 1 < chips)]
    upward = 1 - 2 * (chip % 2)
    acc = (summed, squares)
    mine = data
    other_core = (core + 1) % cores
    received = (lax.ppermute(mine, "chip", exchange), lax.ppermute(mine, "chip", across))
    swapped = lax.ppermute(mine, "core", swap)
    acc = add_pair(acc, swapped, times_listed(chip, other_core))
    for step in range(1, chips):
        if step + 1 == chips:
            acc, received = lax.optimization_barrier((acc, received))
        by_exchange, by_across = received[0], received[-1]
        if step + 2 < chips or (step + 2 == chips and chips < 4):
            received = (lax.ppermute(by_across, "chip", exchange), lax.ppermute(by_exchange, "chip", across))
        elif step + 2 == chips:
            ends = [(chips - 2, chips - 1), (1, 0)]
            part = rows // LAST_PARTS
            received = tuple(
                lax.ppermute(by_across[i * part : (i + 1) * part], "chip", ends) for i in range(LAST_PARTS)
            )
        if step + 1 == chips and chips >= 4:
            far_chip = jnp.where(chip == 0, chips - 1, jnp.where(chip == chips - 1, 0, -1))
            for far in received:
                far_swapped = lax.ppermute(far, "core", swap)
                acc = add_pair(acc, far, times_listed(far_chip, core))
                acc = add_pair(acc, far_swapped, times_listed(far_chip, other_core))
            continue
        exchange_chip = chip + upward * step
        across_chip = chip - upward * step
        exchange_swapped = lax.ppermute(by_exchange, "core", swap)
        across_swapped = lax.ppermute(by_across, "core", swap)
        acc = add_pair(acc, by_exchange, times_listed(exchange_chip, core))
        acc = add_pair(acc, by_across, times_listed(across_chip, core))
        acc = add_pair(acc, exchange_swapped, times_listed(exchange_chip, other_core))
        acc = add_pair(acc, across_swapped, times_listed(across_chip, other_core))
    summed, squares = acc
    result = summed * lax.rsqrt(squares)[:, None] * live[:, None]
    return result.astype(jnp.bfloat16).reshape(1, 1, rows, width)


def solution(mesh):
    devices = mesh.devices
    split = Mesh(
        devices.reshape(devices.shape[0], devices.shape[1] // CORES, CORES),
        ("bucket", "chip", "core"),
    )
    group = ("chip", "core")
    in_specs = (P("bucket", group, None, None, None), P("bucket", group, None, None))
    out_specs = P("bucket", group, None, None)
    return jax.shard_map(
        per_device, mesh=split, in_specs=in_specs, out_specs=out_specs, check_vma=False
    )
```

```python
import jax
import jax.numpy as jnp
from jax import lax
from jax.sharding import Mesh, PartitionSpec as P

ROUNDS = 4


EPS = 1e-06
TEMP = 12.0
DEAD = 1000.0
CORES = 2
LAST_PARTS = 3


def normalize(block):
    values = block.astype(jnp.float32)
    return (values * lax.rsqrt(jnp.sum(values * values, axis=-1, keepdims=True) + EPS)).astype(
        jnp.bfloat16
    )


def weigh(unit_a, unit_b, live_b, extra):
    scores = jnp.dot(unit_a, unit_b.T, preferred_element_type=jnp.float32)
    return jnp.exp(TEMP * scores) * live_b[None, :] * extra


def live_of(block):
    return (block[:, 0] < DEAD / 2).astype(jnp.float32)


def per_device(embeddings, counts):
    buckets = lax.axis_size("bucket")
    bucket = lax.axis_index("bucket")
    slot_rows = embeddings.shape[3]
    width = embeddings.shape[4]
    pieces = embeddings[0, 0]
    slot_index = lax.broadcasted_iota(jnp.int32, pieces.shape, 1)
    lane_index = lax.broadcasted_iota(jnp.int32, pieces.shape, 2)
    dead = (slot_index >= counts[0, 0, :, :, None]) & (lane_index == 0)
    marked = jnp.where(dead, jnp.bfloat16(DEAD), pieces)
    arrived = [lax.dynamic_index_in_dim(marked, bucket, axis=0, keepdims=False)]
    for m in range(1, buckets):
        outgoing = lax.dynamic_index_in_dim(marked, bucket ^ m, axis=0, keepdims=False)
        arrived.append(lax.ppermute(outgoing, "bucket", [(i, i ^ m) for i in range(buckets)]))
    sources = buckets
    rows = sources * slot_rows
    data = jnp.zeros((rows, width), jnp.bfloat16)
    for m, piece in enumerate(arrived):
        data = lax.dynamic_update_slice_in_dim(data, piece, (bucket ^ m) * slot_rows, axis=0)
    live = live_of(data)
    chips = lax.axis_size("chip")
    cores = lax.axis_size("core")
    blocks = chips * cores
    chip = lax.axis_index("chip")
    core = lax.axis_index("core")
    position = chip * cores + core

    unit = normalize(data)
    not_self = 1.0 - jnp.eye(rows, dtype=jnp.float32)
    own = weigh(unit, unit, live, not_self)
    summed = jnp.dot(own.astype(jnp.bfloat16), data, preferred_element_type=jnp.float32)
    squares = jnp.sum(own * own, axis=1)

    def times_listed(other_chip, other_core):
        block = other_chip * cores + other_core
        listed = jnp.int32(0)
        for dist in range(1, ROUNDS + 1):
            for sign in (1, -1):
                listed = listed + (((position + sign * dist) % blocks) == block).astype(jnp.int32)
        exists = (other_chip >= 0) & (other_chip < chips)
        return jnp.where(exists, listed, 0).astype(jnp.float32)

    def pair_terms(acc, got, weight):
        summed, squares = acc
        weights = weigh(unit, normalize(got), live_of(got), 1.0)
        part = jnp.dot(weights.astype(jnp.bfloat16), got, preferred_element_type=jnp.float32)
        return (summed + weight * part, squares + weight * jnp.sum(weights * weights, axis=1))

    def add_pair(acc, got, weight):
        return pair_terms(acc, got, weight)

    swap = [(c, (c + 1) % cores) for c in range(cores)]
    exchange = [(z, z + 1) if z % 2 == 0 else (z, z - 1) for z in range(chips) if z % 2 or z + 1 < chips]
    across = [(z, z - 1) if z % 2 == 0 else (z, z + 1) for z in range(chips) if (z % 2 == 0 and z >= 2) or (z % 2 and z + 1 < chips)]
    upward = 1 - 2 * (chip % 2)
    acc = (summed, squares)
    mine = data
    other_core = (core + 1) % cores
    received = (lax.ppermute(mine, "chip", exchange), lax.ppermute(mine, "chip", across))
    swapped = lax.ppermute(mine, "core", swap)
    acc = add_pair(acc, swapped, times_listed(chip, other_core))
    for step in range(1, chips):
        if step + 1 == chips:
            acc, received = lax.optimization_barrier((acc, received))
        by_exchange, by_across = received[0], received[-1]
        if step + 2 < chips or (step + 2 == chips and chips < 4):
            received = (lax.ppermute(by_across, "chip", exchange), lax.ppermute(by_exchange, "chip", across))
        elif step + 2 == chips:
            ends = [(chips - 2, chips - 1), (1, 0)]
            bounds = [(rows * i // LAST_PARTS) // 16 * 16 for i in range(LAST_PARTS)] + [rows]
            received = tuple(
                lax.ppermute(by_across[bounds[i] : bounds[i + 1]], "chip", ends) for i in range(LAST_PARTS)
            )
        if step + 1 == chips and chips >= 4:
            far_chip = jnp.where(chip == 0, chips - 1, jnp.where(chip == chips - 1, 0, -1))
            for far in received:
                far_swapped = lax.ppermute(far, "core", swap)
                acc = add_pair(acc, far, times_listed(far_chip, core))
                acc = add_pair(acc, far_swapped, times_listed(far_chip, other_core))
            continue
        exchange_chip = chip + upward * step
        across_chip = chip - upward * step
        exchange_swapped = lax.ppermute(by_exchange, "core", swap)
        across_swapped = lax.ppermute(by_across, "core", swap)
        acc = add_pair(acc, by_exchange, times_listed(exchange_chip, core))
        acc = add_pair(acc, by_across, times_listed(across_chip, core))
        acc = add_pair(acc, exchange_swapped, times_listed(exchange_chip, other_core))
        acc = add_pair(acc, across_swapped, times_listed(across_chip, other_core))
    summed, squares = acc
    result = summed * lax.rsqrt(squares)[:, None] * live[:, None]
    return result.astype(jnp.bfloat16).reshape(1, 1, rows, width)


def solution(mesh):
    devices = mesh.devices
    split = Mesh(
        devices.reshape(devices.shape[0], devices.shape[1] // CORES, CORES),
        ("bucket", "chip", "core"),
    )
    group = ("chip", "core")
    in_specs = (P("bucket", group, None, None, None), P("bucket", group, None, None))
    out_specs = P("bucket", group, None, None)
    return jax.shard_map(
        per_device, mesh=split, in_specs=in_specs, out_specs=out_specs, check_vma=False
    )
```

```python
import jax
import jax.numpy as jnp
from jax import lax
from jax.sharding import Mesh, PartitionSpec as P

ROUNDS = 4


EPS = 1e-06
TEMP = 12.0
DEAD = 1000.0
CORES = 2


def normalize(block):
    values = block.astype(jnp.float32)
    return (values * lax.rsqrt(jnp.sum(values * values, axis=-1, keepdims=True) + EPS)).astype(
        jnp.bfloat16
    )


def weigh(unit_a, unit_b, live_b, extra):
    scores = jnp.dot(unit_a, unit_b.T, preferred_element_type=jnp.float32)
    return jnp.exp(TEMP * scores) * live_b[None, :] * extra


def live_of(block):
    return (block[:, 0] < DEAD / 2).astype(jnp.float32)


def per_device(embeddings, counts):
    buckets = lax.axis_size("bucket")
    bucket = lax.axis_index("bucket")
    slot_rows = embeddings.shape[3]
    width = embeddings.shape[4]
    pieces = embeddings[0, 0]
    slot_index = lax.broadcasted_iota(jnp.int32, pieces.shape, 1)
    lane_index = lax.broadcasted_iota(jnp.int32, pieces.shape, 2)
    dead = (slot_index >= counts[0, 0, :, :, None]) & (lane_index == 0)
    marked = jnp.where(dead, jnp.bfloat16(DEAD), pieces)
    arrived = [lax.dynamic_index_in_dim(marked, bucket, axis=0, keepdims=False)]
    for m in range(1, buckets):
        outgoing = lax.dynamic_index_in_dim(marked, bucket ^ m, axis=0, keepdims=False)
        arrived.append(lax.ppermute(outgoing, "bucket", [(i, i ^ m) for i in range(buckets)]))
    sources = buckets
    rows = sources * slot_rows
    data = jnp.zeros((rows, width), jnp.bfloat16)
    for m, piece in enumerate(arrived):
        data = lax.dynamic_update_slice_in_dim(data, piece, (bucket ^ m) * slot_rows, axis=0)
    live = live_of(data)
    chips = lax.axis_size("chip")
    cores = lax.axis_size("core")
    blocks = chips * cores
    chip = lax.axis_index("chip")
    core = lax.axis_index("core")
    position = chip * cores + core

    unit = normalize(data)
    not_self = 1.0 - jnp.eye(rows, dtype=jnp.float32)
    own = weigh(unit, unit, live, not_self)
    summed = jnp.dot(own.astype(jnp.bfloat16), data, preferred_element_type=jnp.float32)
    squares = jnp.sum(own * own, axis=1)

    def times_listed(other_chip, other_core):
        block = other_chip * cores + other_core
        listed = jnp.int32(0)
        for dist in range(1, ROUNDS + 1):
            for sign in (1, -1):
                listed = listed + (((position + sign * dist) % blocks) == block).astype(jnp.int32)
        exists = (other_chip >= 0) & (other_chip < chips)
        return jnp.where(exists, listed, 0).astype(jnp.float32)

    def pair_terms(acc, got, weight):
        summed, squares = acc
        weights = weigh(unit, normalize(got), live_of(got), 1.0)
        part = jnp.dot(weights.astype(jnp.bfloat16), got, preferred_element_type=jnp.float32)
        return (summed + weight * part, squares + weight * jnp.sum(weights * weights, axis=1))

    def add_pair(acc, got, weight):
        return pair_terms(acc, got, weight)

    swap = [(c, (c + 1) % cores) for c in range(cores)]
    exchange = [(z, z + 1) if z % 2 == 0 else (z, z - 1) for z in range(chips) if z % 2 or z + 1 < chips]
    across = [(z, z - 1) if z % 2 == 0 else (z, z + 1) for z in range(chips) if (z % 2 == 0 and z >= 2) or (z % 2 and z + 1 < chips)]
    upward = 1 - 2 * (chip % 2)
    acc = (summed, squares)
    mine = data
    other_core = (core + 1) % cores
    received = (lax.ppermute(mine, "chip", exchange), lax.ppermute(mine, "chip", across))
    swapped = lax.ppermute(mine, "core", swap)
    acc = add_pair(acc, swapped, times_listed(chip, other_core))
    for step in range(1, chips):
        by_exchange, by_across = received
        if step + 2 < chips or (step + 2 == chips and chips < 4):
            received = (lax.ppermute(by_across, "chip", exchange), lax.ppermute(by_exchange, "chip", across))
        elif step + 2 == chips:
            ends = [(chips - 2, chips - 1), (1, 0)]
            half = rows // 2
            received = (
                lax.ppermute(by_across[:half], "chip", ends),
                lax.ppermute(by_across[half:], "chip", ends),
            )
        if step + 1 == chips and chips >= 4:
            far_chip = jnp.where(chip == 0, chips - 1, jnp.where(chip == chips - 1, 0, -1))
            for far in received:
                far_swapped = lax.ppermute(far, "core", swap)
                acc = add_pair(acc, far, times_listed(far_chip, core))
                acc = add_pair(acc, far_swapped, times_listed(far_chip, other_core))
            continue
        exchange_chip = chip + upward * step
        across_chip = chip - upward * step
        exchange_swapped = lax.ppermute(by_exchange, "core", swap)
        across_swapped = lax.ppermute(by_across, "core", swap)
        acc = add_pair(acc, by_exchange, times_listed(exchange_chip, core))
        acc = add_pair(acc, by_across, times_listed(across_chip, core))
        acc = add_pair(acc, exchange_swapped, times_listed(exchange_chip, other_core))
        acc = add_pair(acc, across_swapped, times_listed(across_chip, other_core))
    summed, squares = acc
    result = summed * lax.rsqrt(squares)[:, None] * live[:, None]
    return result.astype(jnp.bfloat16).reshape(1, 1, rows, width)


def solution(mesh):
    devices = mesh.devices
    split = Mesh(
        devices.reshape(devices.shape[0], devices.shape[1] // CORES, CORES),
        ("bucket", "chip", "core"),
    )
    group = ("chip", "core")
    in_specs = (P("bucket", group, None, None, None), P("bucket", group, None, None))
    out_specs = P("bucket", group, None, None)
    return jax.shard_map(
        per_device, mesh=split, in_specs=in_specs, out_specs=out_specs, check_vma=False
    )
```

```python
import jax
import jax.numpy as jnp
from jax import lax
from jax.sharding import Mesh, PartitionSpec as P

ROUNDS = 4


EPS = 1e-06
TEMP = 12.0
DEAD = 1000.0
CORES = 2


def normalize(block):
    values = block.astype(jnp.float32)
    return (values * lax.rsqrt(jnp.sum(values * values, axis=-1, keepdims=True) + EPS)).astype(
        jnp.bfloat16
    )


def weigh(unit_a, unit_b, live_b, extra):
    scores = jnp.dot(unit_a, unit_b.T, preferred_element_type=jnp.float32)
    return jnp.exp(TEMP * scores) * live_b[None, :] * extra


def live_of(block):
    return (block[:, 0] < DEAD / 2).astype(jnp.float32)


def per_device(embeddings, counts):
    buckets = lax.axis_size("bucket")
    bucket = lax.axis_index("bucket")
    slot_rows = embeddings.shape[3]
    width = embeddings.shape[4]
    pieces = embeddings[0, 0]
    slot_index = lax.broadcasted_iota(jnp.int32, pieces.shape, 1)
    lane_index = lax.broadcasted_iota(jnp.int32, pieces.shape, 2)
    dead = (slot_index >= counts[0, 0, :, :, None]) & (lane_index == 0)
    marked = jnp.where(dead, jnp.bfloat16(DEAD), pieces)
    arrived = [lax.dynamic_index_in_dim(marked, bucket, axis=0, keepdims=False)]
    for m in range(1, buckets):
        outgoing = lax.dynamic_index_in_dim(marked, bucket ^ m, axis=0, keepdims=False)
        arrived.append(lax.ppermute(outgoing, "bucket", [(i, i ^ m) for i in range(buckets)]))
    sources = buckets
    rows = sources * slot_rows
    data = jnp.zeros((rows, width), jnp.bfloat16)
    for m, piece in enumerate(arrived):
        data = lax.dynamic_update_slice_in_dim(data, piece, (bucket ^ m) * slot_rows, axis=0)
    live = live_of(data)
    chips = lax.axis_size("chip")
    cores = lax.axis_size("core")
    blocks = chips * cores
    chip = lax.axis_index("chip")
    core = lax.axis_index("core")
    position = chip * cores + core

    unit = normalize(data)
    not_self = 1.0 - jnp.eye(rows, dtype=jnp.float32)
    own = weigh(unit, unit, live, not_self)
    summed = jnp.dot(own.astype(jnp.bfloat16), data, preferred_element_type=jnp.float32)
    squares = jnp.sum(own * own, axis=1)

    def times_listed(other_chip, other_core):
        block = other_chip * cores + other_core
        listed = jnp.int32(0)
        for dist in range(1, ROUNDS + 1):
            for sign in (1, -1):
                listed = listed + (((position + sign * dist) % blocks) == block).astype(jnp.int32)
        exists = (other_chip >= 0) & (other_chip < chips)
        return jnp.where(exists, listed, 0).astype(jnp.float32)

    def pair_terms(acc, got, weight):
        summed, squares = acc
        weights = weigh(unit, normalize(got), live_of(got), 1.0)
        part = jnp.dot(weights.astype(jnp.bfloat16), got, preferred_element_type=jnp.float32)
        return (summed + weight * part, squares + weight * jnp.sum(weights * weights, axis=1))

    def add_pair(acc, got, weight):
        return pair_terms(acc, got, weight)

    swap = [(c, (c + 1) % cores) for c in range(cores)]
    exchange = [(z, z + 1) if z % 2 == 0 else (z, z - 1) for z in range(chips) if z % 2 or z + 1 < chips]
    across = [(z, z - 1) if z % 2 == 0 else (z, z + 1) for z in range(chips) if (z % 2 == 0 and z >= 2) or (z % 2 and z + 1 < chips)]
    upward = 1 - 2 * (chip % 2)
    acc = (summed, squares)
    mine = data
    other_core = (core + 1) % cores
    received = (lax.ppermute(mine, "chip", exchange), lax.ppermute(mine, "chip", across))
    swapped = lax.ppermute(mine, "core", swap)
    acc = add_pair(acc, swapped, times_listed(chip, other_core))
    for step in range(1, chips):
        if step + 1 == chips:
            acc, received = lax.optimization_barrier((acc, received))
        by_exchange, by_across = received[0], received[-1]
        if step + 2 < chips or (step + 2 == chips and chips < 4):
            received = (lax.ppermute(by_across, "chip", exchange), lax.ppermute(by_exchange, "chip", across))
        elif step + 2 == chips:
            ends = [(chips - 2, chips - 1), (1, 0)]
            bounds = [0, rows - rows // 4, rows]
            received = tuple(
                lax.ppermute(by_across[bounds[i] : bounds[i + 1]], "chip", ends) for i in range(len(bounds) - 1)
            )
        if step + 1 == chips and chips >= 4:
            far_chip = jnp.where(chip == 0, chips - 1, jnp.where(chip == chips - 1, 0, -1))
            for far in received:
                far_swapped = lax.ppermute(far, "core", swap)
                acc = add_pair(acc, far, times_listed(far_chip, core))
                acc = add_pair(acc, far_swapped, times_listed(far_chip, other_core))
            continue
        exchange_chip = chip + upward * step
        across_chip = chip - upward * step
        exchange_swapped = lax.ppermute(by_exchange, "core", swap)
        across_swapped = lax.ppermute(by_across, "core", swap)
        acc = add_pair(acc, by_exchange, times_listed(exchange_chip, core))
        acc = add_pair(acc, by_across, times_listed(across_chip, core))
        acc = add_pair(acc, exchange_swapped, times_listed(exchange_chip, other_core))
        acc = add_pair(acc, across_swapped, times_listed(across_chip, other_core))
    summed, squares = acc
    result = summed * lax.rsqrt(squares)[:, None] * live[:, None]
    return result.astype(jnp.bfloat16).reshape(1, 1, rows, width)


def solution(mesh):
    devices = mesh.devices
    split = Mesh(
        devices.reshape(devices.shape[0], devices.shape[1] // CORES, CORES),
        ("bucket", "chip", "core"),
    )
    group = ("chip", "core")
    in_specs = (P("bucket", group, None, None, None), P("bucket", group, None, None))
    out_specs = P("bucket", group, None, None)
    return jax.shard_map(
        per_device, mesh=split, in_specs=in_specs, out_specs=out_specs, check_vma=False
    )
```

```python
import jax
import jax.numpy as jnp
from jax import lax
from jax.sharding import Mesh, PartitionSpec as P

ROUNDS = 4


EPS = 1e-06
TEMP = 12.0
DEAD = 1000.0
CORES = 2


def normalize(block):
    values = block.astype(jnp.float32)
    return (values * lax.rsqrt(jnp.sum(values * values, axis=-1, keepdims=True) + EPS)).astype(
        jnp.bfloat16
    )


def weigh(unit_a, unit_b, live_b, extra):
    scores = jnp.dot(unit_a, unit_b.T, preferred_element_type=jnp.float32)
    return jnp.exp(TEMP * scores) * live_b[None, :] * extra


def live_of(block):
    return (block[:, 0] < DEAD / 2).astype(jnp.float32)


def per_device(embeddings, counts):
    buckets = lax.axis_size("bucket")
    bucket = lax.axis_index("bucket")
    slot_rows = embeddings.shape[3]
    width = embeddings.shape[4]
    pieces = embeddings[0, 0]
    slot_index = lax.broadcasted_iota(jnp.int32, pieces.shape, 1)
    lane_index = lax.broadcasted_iota(jnp.int32, pieces.shape, 2)
    dead = (slot_index >= counts[0, 0, :, :, None]) & (lane_index == 0)
    marked = jnp.where(dead, jnp.bfloat16(DEAD), pieces)
    arrived = [lax.dynamic_index_in_dim(marked, bucket, axis=0, keepdims=False)]
    for m in range(1, buckets):
        outgoing = lax.dynamic_index_in_dim(marked, bucket ^ m, axis=0, keepdims=False)
        arrived.append(lax.ppermute(outgoing, "bucket", [(i, i ^ m) for i in range(buckets)]))
    sources = buckets
    rows = sources * slot_rows
    data = jnp.zeros((rows, width), jnp.bfloat16)
    for m, piece in enumerate(arrived):
        data = lax.dynamic_update_slice_in_dim(data, piece, (bucket ^ m) * slot_rows, axis=0)
    live = live_of(data)
    chips = lax.axis_size("chip")
    cores = lax.axis_size("core")
    blocks = chips * cores
    chip = lax.axis_index("chip")
    core = lax.axis_index("core")
    position = chip * cores + core

    unit = normalize(data)
    not_self = 1.0 - jnp.eye(rows, dtype=jnp.float32)
    own = weigh(unit, unit, live, not_self)
    summed = jnp.dot(own.astype(jnp.bfloat16), data, preferred_element_type=jnp.float32)
    squares = jnp.sum(own * own, axis=1)

    def times_listed(other_chip, other_core):
        block = other_chip * cores + other_core
        listed = jnp.int32(0)
        for dist in range(1, ROUNDS + 1):
            for sign in (1, -1):
                listed = listed + (((position + sign * dist) % blocks) == block).astype(jnp.int32)
        exists = (other_chip >= 0) & (other_chip < chips)
        return jnp.where(exists, listed, 0).astype(jnp.float32)

    def pair_terms(acc, got, weight):
        summed, squares = acc
        weights = weigh(unit, normalize(got), live_of(got), 1.0)
        part = jnp.dot(weights.astype(jnp.bfloat16), got, preferred_element_type=jnp.float32)
        return (summed + weight * part, squares + weight * jnp.sum(weights * weights, axis=1))

    def add_pair(acc, got, weight):
        return pair_terms(acc, got, weight)

    swap = [(c, (c + 1) % cores) for c in range(cores)]
    exchange = [(z, z + 1) if z % 2 == 0 else (z, z - 1) for z in range(chips) if z % 2 or z + 1 < chips]
    across = [(z, z - 1) if z % 2 == 0 else (z, z + 1) for z in range(chips) if (z % 2 == 0 and z >= 2) or (z % 2 and z + 1 < chips)]
    upward = 1 - 2 * (chip % 2)
    acc = (summed, squares)
    mine = data
    other_core = (core + 1) % cores
    received = (lax.ppermute(mine, "chip", exchange), lax.ppermute(mine, "chip", across))
    swapped = lax.ppermute(mine, "core", swap)
    acc = add_pair(acc, swapped, times_listed(chip, other_core))
    for step in range(1, chips):
        if step + 1 == chips:
            acc, received = lax.optimization_barrier((acc, received))
        by_exchange, by_across = received[0], received[-1]
        if step + 2 < chips or (step + 2 == chips and chips < 4):
            received = (lax.ppermute(by_across, "chip", exchange), lax.ppermute(by_exchange, "chip", across))
        elif step + 2 == chips:
            ends = [(chips - 2, chips - 1), (1, 0)]
            bounds = [0, rows - rows // 8, rows]
            received = tuple(
                lax.ppermute(by_across[bounds[i] : bounds[i + 1]], "chip", ends) for i in range(len(bounds) - 1)
            )
        if step + 1 == chips and chips >= 4:
            far_chip = jnp.where(chip == 0, chips - 1, jnp.where(chip == chips - 1, 0, -1))
            for far in received:
                far_swapped = lax.ppermute(far, "core", swap)
                acc = add_pair(acc, far, times_listed(far_chip, core))
                acc = add_pair(acc, far_swapped, times_listed(far_chip, other_core))
            continue
        exchange_chip = chip + upward * step
        across_chip = chip - upward * step
        exchange_swapped = lax.ppermute(by_exchange, "core", swap)
        across_swapped = lax.ppermute(by_across, "core", swap)
        acc = add_pair(acc, by_exchange, times_listed(exchange_chip, core))
        acc = add_pair(acc, by_across, times_listed(across_chip, core))
        acc = add_pair(acc, exchange_swapped, times_listed(exchange_chip, other_core))
        acc = add_pair(acc, across_swapped, times_listed(across_chip, other_core))
    summed, squares = acc
    result = summed * lax.rsqrt(squares)[:, None] * live[:, None]
    return result.astype(jnp.bfloat16).reshape(1, 1, rows, width)


def solution(mesh):
    devices = mesh.devices
    split = Mesh(
        devices.reshape(devices.shape[0], devices.shape[1] // CORES, CORES),
        ("bucket", "chip", "core"),
    )
    group = ("chip", "core")
    in_specs = (P("bucket", group, None, None, None), P("bucket", group, None, None))
    out_specs = P("bucket", group, None, None)
    return jax.shard_map(
        per_device, mesh=split, in_specs=in_specs, out_specs=out_specs, check_vma=False
    )
```

```python
import jax
import jax.numpy as jnp
from jax import lax
from jax.sharding import Mesh, PartitionSpec as P

ROUNDS = 4


EPS = 1e-06
TEMP = 12.0
DEAD = 1000.0
CORES = 2


def normalize(block):
    values = block.astype(jnp.float32)
    return (values * lax.rsqrt(jnp.sum(values * values, axis=-1, keepdims=True) + EPS)).astype(
        jnp.bfloat16
    )


def weigh(unit_a, unit_b, live_b, extra):
    scores = jnp.dot(unit_a, unit_b.T, preferred_element_type=jnp.float32)
    return jnp.exp(TEMP * scores) * live_b[None, :] * extra


def live_of(block):
    return (block[:, 0] < DEAD / 2).astype(jnp.float32)


def per_device(embeddings, counts):
    buckets = lax.axis_size("bucket")
    bucket = lax.axis_index("bucket")
    slot_rows = embeddings.shape[3]
    width = embeddings.shape[4]
    pieces = embeddings[0, 0]
    slot_index = lax.broadcasted_iota(jnp.int32, pieces.shape, 1)
    lane_index = lax.broadcasted_iota(jnp.int32, pieces.shape, 2)
    dead = (slot_index >= counts[0, 0, :, :, None]) & (lane_index == 0)
    marked = jnp.where(dead, jnp.bfloat16(DEAD), pieces)
    arrived = [lax.dynamic_index_in_dim(marked, bucket, axis=0, keepdims=False)]
    for m in range(1, buckets):
        outgoing = lax.dynamic_index_in_dim(marked, bucket ^ m, axis=0, keepdims=False)
        arrived.append(lax.ppermute(outgoing, "bucket", [(i, i ^ m) for i in range(buckets)]))
    sources = buckets
    rows = sources * slot_rows
    data = jnp.zeros((rows, width), jnp.bfloat16)
    for m, piece in enumerate(arrived):
        data = lax.dynamic_update_slice_in_dim(data, piece, (bucket ^ m) * slot_rows, axis=0)
    live = live_of(data)
    chips = lax.axis_size("chip")
    cores = lax.axis_size("core")
    blocks = chips * cores
    chip = lax.axis_index("chip")
    core = lax.axis_index("core")
    position = chip * cores + core

    unit = normalize(data)
    not_self = 1.0 - jnp.eye(rows, dtype=jnp.float32)
    own = weigh(unit, unit, live, not_self)
    summed = jnp.dot(own.astype(jnp.bfloat16), data, preferred_element_type=jnp.float32)
    squares = jnp.sum(own * own, axis=1)

    def times_listed(other_chip, other_core):
        block = other_chip * cores + other_core
        listed = jnp.int32(0)
        for dist in range(1, ROUNDS + 1):
            for sign in (1, -1):
                listed = listed + (((position + sign * dist) % blocks) == block).astype(jnp.int32)
        exists = (other_chip >= 0) & (other_chip < chips)
        return jnp.where(exists, listed, 0).astype(jnp.float32)

    def pair_terms(acc, got, weight):
        summed, squares = acc
        weights = weigh(unit, normalize(got), live_of(got), 1.0)
        part = jnp.dot(weights.astype(jnp.bfloat16), got, preferred_element_type=jnp.float32)
        return (summed + weight * part, squares + weight * jnp.sum(weights * weights, axis=1))

    def add_pair(acc, got, weight):
        return pair_terms(acc, got, weight)

    swap = [(c, (c + 1) % cores) for c in range(cores)]
    exchange = [(z, z + 1) if z % 2 == 0 else (z, z - 1) for z in range(chips) if z % 2 or z + 1 < chips]
    across = [(z, z - 1) if z % 2 == 0 else (z, z + 1) for z in range(chips) if (z % 2 == 0 and z >= 2) or (z % 2 and z + 1 < chips)]
    upward = 1 - 2 * (chip % 2)
    acc = (summed, squares)
    mine = data
    other_core = (core + 1) % cores
    received = (lax.ppermute(mine, "chip", exchange), lax.ppermute(mine, "chip", across))
    swapped = lax.ppermute(mine, "core", swap)
    acc = add_pair(acc, swapped, times_listed(chip, other_core))
    for step in range(1, chips):
        if step + 1 == chips:
            acc, received = lax.optimization_barrier((acc, received))
        by_exchange, by_across = received[0], received[-1]
        if step + 2 < chips or (step + 2 == chips and chips < 4):
            received = (lax.ppermute(by_across, "chip", exchange), lax.ppermute(by_exchange, "chip", across))
        elif step + 2 == chips:
            ends = [(chips - 2, chips - 1), (1, 0)]
            bounds = [0, rows - 3 * rows // 16, rows]
            received = tuple(
                lax.ppermute(by_across[bounds[i] : bounds[i + 1]], "chip", ends) for i in range(len(bounds) - 1)
            )
        if step + 1 == chips and chips >= 4:
            far_chip = jnp.where(chip == 0, chips - 1, jnp.where(chip == chips - 1, 0, -1))
            for far in received:
                far_swapped = lax.ppermute(far, "core", swap)
                acc = add_pair(acc, far, times_listed(far_chip, core))
                acc = add_pair(acc, far_swapped, times_listed(far_chip, other_core))
            continue
        exchange_chip = chip + upward * step
        across_chip = chip - upward * step
        exchange_swapped = lax.ppermute(by_exchange, "core", swap)
        across_swapped = lax.ppermute(by_across, "core", swap)
        acc = add_pair(acc, by_exchange, times_listed(exchange_chip, core))
        acc = add_pair(acc, by_across, times_listed(across_chip, core))
        acc = add_pair(acc, exchange_swapped, times_listed(exchange_chip, other_core))
        acc = add_pair(acc, across_swapped, times_listed(across_chip, other_core))
    summed, squares = acc
    result = summed * lax.rsqrt(squares)[:, None] * live[:, None]
    return result.astype(jnp.bfloat16).reshape(1, 1, rows, width)


def solution(mesh):
    devices = mesh.devices
    split = Mesh(
        devices.reshape(devices.shape[0], devices.shape[1] // CORES, CORES),
        ("bucket", "chip", "core"),
    )
    group = ("chip", "core")
    in_specs = (P("bucket", group, None, None, None), P("bucket", group, None, None))
    out_specs = P("bucket", group, None, None)
    return jax.shard_map(
        per_device, mesh=split, in_specs=in_specs, out_specs=out_specs, check_vma=False
    )
```
